256 devices in a mesh: dp: 16 (over z, core), seq: 16 (over y, x).
Axes of the slice: x: 4, y: 4, z: 8, core: 2. Of those that a mesh axis runs over, the one named last changes fastest.
Arguments:
- queries: bfloat16 [16, 16, 144, 1536], P('dp', 'seq'), may hold values from -32 to 32
- keys: bfloat16 [16, 16, 144, 1536], P('dp', 'seq'), may hold values from -32 to 32
- values: bfloat16 [16, 16, 144, 1536], P('dp', 'seq'), may hold values from -6 to 6
- cotangent: bfloat16 [16, 16, 144, 1536], P('dp', 'seq'), may hold values from -6 to 6
- spatial_count: int32 [16, 16], P('dp', 'seq'), may hold values from 72 to 144, as said below
- clip_ids: int32 [16, 16], P('dp'), may hold values from 0 to 1, never falling along the last dimension, each value on 1 to 12 neighbouring positions
- time_bias: float32 [12, 16], replicated, may hold values from -4 to 4
Outputs:
- attended: bfloat16 [16, 16, 144, 1536], P('dp', 'seq')
- query_grad: bfloat16 [16, 16, 144, 1536], P('dp', 'seq')
- key_grad: bfloat16 [16, 16, 144, 1536], P('dp', 'seq')
- value_grad: bfloat16 [16, 16, 144, 1536], P('dp', 'seq')
- bias_grad: float32 [12, 16], replicated
The draws below stay inside these ranges and needn't reach their ends.
Inputs may be any that keep to these rules, and one draw needn't show every extreme that they name: The live spatial tokens of a frame are its first spatial_count positions; in each group some frame has all 144 live. `clip_ids`: frames of one clip are consecutive; a clip has at most 12 frames.
All inputs are finite; a program needn't handle non-finite values.
Results may differ from the reference program's by a relative error of at most 0.0059.
Values may be sent and summed in bfloat16 or wider, within the bound.
No kernel may reach another device: no remote copies, remote signals or barrier semaphores. Data moves between devices by JAX's collectives and lax.ppermute only.
A program may use at most 64 MiB of HBM per device.

```python
import math
import jax
import jax.numpy as jnp
import numpy as np
from jax import lax

HEADS = 12
HEAD = 128
P_SIZE = 144
FR_DEV = 1
CLIPS = 2
GROUPS = 16
FT = 16
N_SEQ = 16


def paired_fields(key):
    full_shape = (GROUPS, FT, P_SIZE, HEADS * HEAD)
    folded = jax.random.fold_in(key, 4057)
    streams = jax.random.split(folded, 2)
    query_field = jnp.clip(jax.random.normal(streams[0], full_shape, jnp.float32), -6.0, 6.0)
    key_field = jnp.clip(jax.random.normal(streams[1], full_shape, jnp.float32), -6.0, 6.0)
    return (query_field, key_field)


def draw_queries(key, part):
    return paired_fields(key)[0].astype(jnp.bfloat16)


def draw_keys(key, part):
    return paired_fields(key)[1].astype(jnp.bfloat16)


def draw_spatial_count(key, part):
    streams = jax.random.split(jax.random.fold_in(key, 313), 2)
    counts = jax.random.randint(streams[0], (GROUPS, FT), P_SIZE // 2, P_SIZE + 1, dtype=jnp.int32)
    full_frame = jax.random.randint(streams[1], (GROUPS, 1), 0, FT, dtype=jnp.int32)
    frame_index = lax.broadcasted_iota(jnp.int32, (GROUPS, FT), 1)
    return jnp.where(frame_index == full_frame, P_SIZE, counts).astype(jnp.int32)


def steps_of(own_key, shape, cuts, least, largest):
    def one(dim, blocks):
        draws = jax.random.uniform(jax.random.fold_in(jax.random.fold_in(own_key, 6), dim), (blocks,), jnp.float32, least / len(cuts), largest / len(cuts))
        return jnp.repeat(jnp.exp(draws), shape[dim] // blocks).reshape((-1,) + (1,) * (len(shape) - dim - 1))

    level = one(*cuts[0])
    for cut in cuts[1:]:
        level = level * one(*cut)
    return level


def profile(amount, total, limit, lean):
    weights = [(1 << 20) // math.isqrt(grade ** lean) + 1 for grade in range(2, amount + 1)]
    rest, holding = total - limit - (amount - 1), [1] * (amount - 1)
    while rest > 0:
        movable = [i for i in range(amount - 1) if holding[i] < limit]
        pool, budget = sum([weights[i] for i in movable]), rest
        for i in movable:
            addition = min(limit - holding[i], max(1, budget * weights[i] // pool), rest)
            holding[i] = holding[i] + addition
            rest = rest - addition
    return np.array([limit] + holding)


def uneven(key, amount, total, bound, lean):
    if amount == 2:
        one = jax.random.randint(key, (), max(1, total - bound), min(bound, total - 1) + 1)
        return jnp.stack([one, total - one])
    tallies = jnp.asarray(profile(amount, total, bound, lean), jnp.int32)
    twos = (amount - 1) // 2
    giver, taker = tallies[1:1 + 2 * twos:2], tallies[2:2 + 2 * twos:2]
    slack = jnp.minimum(giver - 1, bound - taker)
    moved = jax.random.randint(jax.random.fold_in(key, 1), (twos,), 0, 1 << 20) % (slack + 1)
    tallies = tallies.at[1:1 + 2 * twos:2].set(giver - moved).at[2:2 + 2 * twos:2].set(taker + moved)
    return tallies[jax.random.permutation(jax.random.fold_in(key, 2), amount)]


def centred(own_key, shape, scale, limit, cuts=(), kind=jnp.bfloat16):
    values = jax.random.normal(own_key, shape, jnp.float32) * scale
    if len(cuts) > 0:
        values = steps_of(own_key, shape, cuts, -0.22, 0.18) * values
    return jnp.clip(values, min=-limit, max=limit).astype(kind)


def setup_inputs(seed: int = 0) -> dict:
    key_list = jax.random.split(jax.random.key(seed), 8)
    queries = draw_queries(jax.random.fold_in(key_list[7], 71), 0)
    keys = draw_keys(jax.random.fold_in(key_list[7], 71), 0)
    values = centred(key_list[2], (GROUPS, FT, P_SIZE, HEADS * HEAD), 1.0, 6.0, ((0, 16), (1, 16)))
    cotangent = centred(key_list[3], (GROUPS, FT, P_SIZE, HEADS * HEAD), 1.0, 6.0, ((0, 16), (1, 16)))
    spatial_count = draw_spatial_count(jax.random.fold_in(key_list[7], 71), 0)
    clip_ids = jax.vmap(lambda own: jnp.searchsorted(jnp.cumsum(uneven(own, CLIPS, FT, 3 * FR_DEV * N_SEQ // 4, 2)), jnp.arange(FT), side="right"))(jax.random.split(key_list[5], GROUPS)).reshape((GROUPS, FT)).astype(jnp.int32)
    time_bias = centred(key_list[6], (HEADS, FT), 1.0, 4.0, (), jnp.float32)
    return {"queries": queries, "keys": keys, "values": values, "cotangent": cotangent, "spatial_count": spatial_count, "clip_ids": clip_ids, "time_bias": time_bias}


SPACE_PATTERNS = ('bfihe,bfjhe->bfhij', 'bfhij,bfjhe->bfihe', 'bfhij,bfihe->bfjhe')
TIME_PATTERNS = ('biphe,bjphe->bphij', 'bphij,bjphe->biphe', 'bphij,biphe->bjphe')

def split_heads(tensor):
    return tensor.reshape(tensor.shape[:-1] + (HEADS, HEAD)).astype(jnp.float32)

def rounded(tensor):
    return lax.optimization_barrier(tensor.astype(jnp.bfloat16)).astype(jnp.float32)

def attend_pair(patterns, query_part, key_part, value_part, cotangent_part, bias, allowed):
    scaling = 1.0 / math.sqrt(HEAD)
    scores = jnp.einsum(patterns[0], query_part, key_part) * scaling + bias
    scores = jnp.where(allowed, scores, -1e+30)
    row_peak = lax.optimization_barrier(jnp.max(scores, axis=-1, keepdims=True))
    weights = jnp.exp(scores - row_peak)
    shares = weights / lax.optimization_barrier(jnp.sum(weights, axis=-1, keepdims=True))
    shares_half = rounded(shares)
    result = jnp.einsum(patterns[1], shares_half, value_part)
    value_grad = jnp.einsum(patterns[2], shares_half, cotangent_part)
    share_grad = jnp.einsum(patterns[0], cotangent_part, value_part)
    spread = lax.optimization_barrier(jnp.sum(shares * share_grad, axis=-1, keepdims=True))
    score_grad = shares * (share_grad - spread)
    score_half = rounded(score_grad)
    query_grad = jnp.einsum(patterns[1], score_half, key_part) * scaling
    key_grad = jnp.einsum(patterns[2], score_half, query_part) * scaling
    return (result, query_grad, key_grad, value_grad, score_grad)

def reference(queries, keys, values, cotangent, spatial_count, clip_ids, time_bias):
    row_index = lax.broadcasted_iota(jnp.int32, (FT, FT), 0)
    col_index = lax.broadcasted_iota(jnp.int32, (FT, FT), 1)
    distance = jnp.abs(row_index - col_index)
    lag_index = lax.broadcasted_iota(jnp.int32, (FT, FT, FT), 0)
    onehot = (lag_index == distance[None]).astype(jnp.float32)
    bias_table = jnp.tensordot(time_bias, onehot, axes=1, precision=lax.Precision.HIGHEST)[None, None]

    def one_group(pieces):
        query_field, key_field, value_field, cotangent_field, live_count, clip_row = pieces
        query_part = split_heads(query_field[None])
        key_part = split_heads(key_field[None])
        value_part = split_heads(value_field[None])
        cotangent_part = split_heads(cotangent_field[None])
        position = lax.broadcasted_iota(jnp.int32, (1, 1, 1, 1, P_SIZE), 4)
        live_keys = position < live_count.astype(jnp.int32)[None, :, None, None, None]
        space = attend_pair(SPACE_PATTERNS, query_part, key_part, value_part, cotangent_part, 0.0, live_keys)
        same_clip = (clip_row[:, None] == clip_row[None, :])[None, None, None]
        timing = attend_pair(TIME_PATTERNS, query_part, key_part, value_part, cotangent_part, bias_table, same_clip)
        width = HEADS * HEAD
        attended = (space[0] + rounded(timing[0])).astype(jnp.bfloat16).reshape(FT, P_SIZE, width)
        query_grad = (space[1] + rounded(timing[1])).astype(jnp.bfloat16).reshape(FT, P_SIZE, width)
        key_grad = (space[2] + rounded(timing[2])).astype(jnp.bfloat16).reshape(FT, P_SIZE, width)
        value_grad = (space[3] + rounded(timing[3])).astype(jnp.bfloat16).reshape(FT, P_SIZE, width)
        bias_part = jnp.tensordot(lax.optimization_barrier(jnp.sum(timing[4], axis=(0, 1))), onehot, axes=((1, 2), (1, 2)), precision=lax.Precision.HIGHEST)
        return (attended, query_grad, key_grad, value_grad, bias_part)
    outputs = lax.map(one_group, (queries, keys, values, cotangent, spatial_count, clip_ids))
    bias_grad = lax.optimization_barrier(jnp.sum(outputs[4], axis=0)) / math.sqrt(GROUPS * FT * P_SIZE)
    return (outputs[0], outputs[1], outputs[2], outputs[3], bias_grad)
```

```python
import math

import jax
import jax.numpy as jnp
from jax import lax
from jax.sharding import PartitionSpec as P

SPACE_PATTERNS = ("bfihe,bfjhe->bfhij", "bfhij,bfjhe->bfihe", "bfhij,bfihe->bfjhe")
TIME_PATTERNS = ("biphe,bjphe->bphij", "bphij,bjphe->biphe", "bphij,biphe->bjphe")


def split_heads(tensor, head_count):
    return tensor.reshape(tensor.shape[:-1] + (head_count, tensor.shape[-1] // head_count))


def join_heads(tensor):
    return tensor.reshape(tensor.shape[:-2] + (tensor.shape[-2] * tensor.shape[-1],))


def attend_forward(patterns, query_part, key_part, value_part, bias, allowed):
    scaling = 1.0 / math.sqrt(query_part.shape[-1])
    scores = (
        jnp.einsum(patterns[0], query_part, key_part, preferred_element_type=jnp.float32) * scaling
        + bias
    )
    scores = jnp.where(allowed, scores, -1e30)
    row_peak = jnp.max(scores, axis=-1, keepdims=True)
    weights = jnp.exp(scores - row_peak)
    shares = weights / jnp.sum(weights, axis=-1, keepdims=True)
    shares_half = shares.astype(jnp.bfloat16)
    result = jnp.einsum(patterns[1], shares_half, value_part, preferred_element_type=jnp.float32)
    return (shares, shares_half, result)


def attend_backward(
    patterns, query_part, key_part, value_part, cotangent_part, shares, shares_half
):
    scaling = 1.0 / math.sqrt(query_part.shape[-1])
    value_grad = jnp.einsum(
        patterns[2], shares_half, cotangent_part, preferred_element_type=jnp.float32
    )
    share_grad = jnp.einsum(
        patterns[0], cotangent_part, value_part, preferred_element_type=jnp.float32
    )
    spread = jnp.sum(shares * share_grad, axis=-1, keepdims=True)
    score_grad = shares * (share_grad - spread)
    score_half = score_grad.astype(jnp.bfloat16)
    query_grad = (
        jnp.einsum(patterns[1], score_half, key_part, preferred_element_type=jnp.float32) * scaling
    )
    key_grad = (
        jnp.einsum(patterns[2], score_half, query_part, preferred_element_type=jnp.float32)
        * scaling
    )
    return (query_grad, key_grad, value_grad, score_grad)


def butterfly_sum(value, axis, size):
    step = 1
    while step < size:
        pairs = [(index, index ^ step) for index in range(size)]
        value = value + lax.ppermute(value, axis, pairs)
        step *= 2
    return value


def on_device(queries, keys, values, cotangent, spatial_count, clip_ids, time_bias):
    head_count, frames_all = time_bias.shape
    positions = queries.shape[2]
    width = queries.shape[3]
    seq_size = lax.axis_size("seq")
    dp_size = lax.axis_size("dp")
    row_index = lax.broadcasted_iota(jnp.int32, (frames_all, frames_all), 0)
    col_index = lax.broadcasted_iota(jnp.int32, (frames_all, frames_all), 1)
    distance = jnp.abs(row_index - col_index)
    lag_index = lax.broadcasted_iota(jnp.int32, (frames_all, frames_all, frames_all), 0)
    onehot = (lag_index == distance[None]).astype(jnp.float32)
    bias_table = jnp.tensordot(time_bias, onehot, axes=1, precision=lax.Precision.HIGHEST)[
        None, None
    ]
    same_clip = (clip_ids[:, :, None] == clip_ids[:, None, :])[:, None, None]
    position = lax.broadcasted_iota(jnp.int32, (1, 1, 1, 1, positions), 4)
    live_keys = position < spatial_count[:, :, None, None, None]

    block = positions // seq_size
    stacked = jnp.stack([queries[0, 0], keys[0, 0], values[0, 0], cotangent[0, 0]])
    stacked = stacked.reshape(4, seq_size, block, width)
    rows = lax.all_to_all(stacked, "seq", split_axis=1, concat_axis=1, tiled=True)
    query_part = split_heads(rows[0][None], head_count)
    key_part = split_heads(rows[1][None], head_count)
    value_part = split_heads(rows[2][None], head_count)
    slope_part = split_heads(rows[3][None], head_count)
    shares, shares_half, result = attend_forward(
        TIME_PATTERNS, query_part, key_part, value_part, bias_table, same_clip
    )
    time_grads = attend_backward(
        TIME_PATTERNS, query_part, key_part, value_part, slope_part, shares, shares_half
    )
    bias_part = jnp.tensordot(
        jnp.sum(time_grads[3], axis=(0, 1)),
        onehot,
        axes=((1, 2), (1, 2)),
        precision=lax.Precision.HIGHEST,
    )
    summed = butterfly_sum(butterfly_sum(bias_part, "seq", seq_size), "dp", dp_size)
    bias_grad = summed / math.sqrt(dp_size * queries.shape[0] * frames_all * positions)

    back_rows = jnp.stack(
        [
            join_heads(result[0]).astype(jnp.bfloat16),
            join_heads(time_grads[0][0]).astype(jnp.bfloat16),
            join_heads(time_grads[1][0]).astype(jnp.bfloat16),
            join_heads(time_grads[2][0]).astype(jnp.bfloat16),
        ]
    )
    back = lax.all_to_all(back_rows, "seq", split_axis=1, concat_axis=2, tiled=True)
    back = back.reshape(4, 1, 1, positions, width).astype(jnp.float32)

    space_query = split_heads(queries, head_count)
    space_key = split_heads(keys, head_count)
    space_value = split_heads(values, head_count)
    space_slope = split_heads(cotangent, head_count)
    space_shares, space_half, space_out = attend_forward(
        SPACE_PATTERNS, space_query, space_key, space_value, 0.0, live_keys
    )
    space_grads = attend_backward(
        SPACE_PATTERNS, space_query, space_key, space_value, space_slope, space_shares, space_half
    )
    attended = (join_heads(space_out) + back[0]).astype(jnp.bfloat16)
    query_grad = (join_heads(space_grads[0]) + back[1]).astype(jnp.bfloat16)
    key_grad = (join_heads(space_grads[1]) + back[2]).astype(jnp.bfloat16)
    value_grad = (join_heads(space_grads[2]) + back[3]).astype(jnp.bfloat16)
    return (attended, query_grad, key_grad, value_grad, bias_grad)


def solution(mesh):
    return jax.shard_map(
        on_device,
        mesh=mesh,
        in_specs=(
            P("dp", "seq", None, None),
            P("dp", "seq", None, None),
            P("dp", "seq", None, None),
            P("dp", "seq", None, None),
            P("dp", "seq"),
            P("dp", None),
            P(),
        ),
        out_specs=(
            P("dp", "seq", None, None),
            P("dp", "seq", None, None),
            P("dp", "seq", None, None),
            P("dp", "seq", None, None),
            P(),
        ),
        check_vma=False,
    )
```

```python
import math

import jax
import jax.numpy as jnp
from jax import lax
from jax.sharding import PartitionSpec as P

SPACE_PATTERNS = ("bfihe,bfjhe->bfhij", "bfhij,bfjhe->bfihe", "bfhij,bfihe->bfjhe")
TIME_PATTERNS = ("biphe,bjphe->bphij", "bphij,bjphe->biphe", "bphij,biphe->bjphe")


def split_heads(tensor, head_count):
    return tensor.reshape(tensor.shape[:-1] + (head_count, tensor.shape[-1] // head_count))


def join_heads(tensor):
    return tensor.reshape(tensor.shape[:-2] + (tensor.shape[-2] * tensor.shape[-1],))


def attend_forward(patterns, query_part, key_part, value_part, bias, allowed):
    scaling = 1.0 / math.sqrt(query_part.shape[-1])
    scores = (
        jnp.einsum(patterns[0], query_part, key_part, preferred_element_type=jnp.float32) * scaling
        + bias
    )
    scores = jnp.where(allowed, scores, -1e30)
    row_peak = jnp.max(scores, axis=-1, keepdims=True)
    weights = jnp.exp(scores - row_peak)
    shares = weights / jnp.sum(weights, axis=-1, keepdims=True)
    shares_half = shares.astype(jnp.bfloat16)
    result = jnp.einsum(patterns[1], shares_half, value_part, preferred_element_type=jnp.float32)
    return (shares, shares_half, result)


def attend_backward(
    patterns, query_part, key_part, value_part, cotangent_part, shares, shares_half
):
    scaling = 1.0 / math.sqrt(query_part.shape[-1])
    value_grad = jnp.einsum(
        patterns[2], shares_half, cotangent_part, preferred_element_type=jnp.float32
    )
    share_grad = jnp.einsum(
        patterns[0], cotangent_part, value_part, preferred_element_type=jnp.float32
    )
    spread = jnp.sum(shares * share_grad, axis=-1, keepdims=True)
    score_grad = shares * (share_grad - spread)
    score_half = score_grad.astype(jnp.bfloat16)
    query_grad = (
        jnp.einsum(patterns[1], score_half, key_part, preferred_element_type=jnp.float32) * scaling
    )
    key_grad = (
        jnp.einsum(patterns[2], score_half, query_part, preferred_element_type=jnp.float32)
        * scaling
    )
    return (query_grad, key_grad, value_grad, score_grad)


def gathered_sum(value, axis, size):
    me = lax.axis_index(axis)
    received = [value]
    for shift in range(1, size):
        pairs = [(index, (index + shift) % size) for index in range(size)]
        received.append(lax.ppermute(value, axis, pairs))
    received = jnp.stack(received)
    by_source = jnp.take(received, (me - jnp.arange(size)) % size, axis=0)
    total = by_source[0]
    for source in range(1, size):
        total = total + by_source[source]
    return total


def on_device(queries, keys, values, cotangent, spatial_count, clip_ids, time_bias):
    head_count, frames_all = time_bias.shape
    positions = queries.shape[2]
    width = queries.shape[3]
    seq_size = lax.axis_size("seq")
    dp_size = lax.axis_size("dp")
    row_index = lax.broadcasted_iota(jnp.int32, (frames_all, frames_all), 0)
    col_index = lax.broadcasted_iota(jnp.int32, (frames_all, frames_all), 1)
    distance = jnp.abs(row_index - col_index)
    lag_index = lax.broadcasted_iota(jnp.int32, (frames_all, frames_all, frames_all), 0)
    onehot = (lag_index == distance[None]).astype(jnp.float32)
    bias_table = jnp.tensordot(time_bias, onehot, axes=1, precision=lax.Precision.HIGHEST)[
        None, None
    ]
    same_clip = (clip_ids[:, :, None] == clip_ids[:, None, :])[:, None, None]
    position = lax.broadcasted_iota(jnp.int32, (1, 1, 1, 1, positions), 4)
    live_keys = position < spatial_count[:, :, None, None, None]

    block = positions // seq_size
    stacked = jnp.stack([queries[0, 0], keys[0, 0], values[0, 0], cotangent[0, 0]])
    stacked = stacked.reshape(4, seq_size, block, width)
    rows = lax.all_to_all(stacked, "seq", split_axis=1, concat_axis=1, tiled=True)
    query_part = split_heads(rows[0][None], head_count)
    key_part = split_heads(rows[1][None], head_count)
    value_part = split_heads(rows[2][None], head_count)
    slope_part = split_heads(rows[3][None], head_count)
    shares, shares_half, result = attend_forward(
        TIME_PATTERNS, query_part, key_part, value_part, bias_table, same_clip
    )
    time_grads = attend_backward(
        TIME_PATTERNS, query_part, key_part, value_part, slope_part, shares, shares_half
    )
    bias_part = jnp.tensordot(
        jnp.sum(time_grads[3], axis=(0, 1)),
        onehot,
        axes=((1, 2), (1, 2)),
        precision=lax.Precision.HIGHEST,
    )
    summed = gathered_sum(gathered_sum(bias_part, "seq", seq_size), "dp", dp_size)
    bias_grad = summed / math.sqrt(dp_size * queries.shape[0] * frames_all * positions)

    back_rows = jnp.stack(
        [
            join_heads(result[0]).astype(jnp.bfloat16),
            join_heads(time_grads[0][0]).astype(jnp.bfloat16),
            join_heads(time_grads[1][0]).astype(jnp.bfloat16),
            join_heads(time_grads[2][0]).astype(jnp.bfloat16),
        ]
    )
    back = lax.all_to_all(back_rows, "seq", split_axis=1, concat_axis=2, tiled=True)
    back = back.reshape(4, 1, 1, positions, width).astype(jnp.float32)

    space_query = split_heads(queries, head_count)
    space_key = split_heads(keys, head_count)
    space_value = split_heads(values, head_count)
    space_slope = split_heads(cotangent, head_count)
    space_shares, space_half, space_out = attend_forward(
        SPACE_PATTERNS, space_query, space_key, space_value, 0.0, live_keys
    )
    space_grads = attend_backward(
        SPACE_PATTERNS, space_query, space_key, space_value, space_slope, space_shares, space_half
    )
    attended = (join_heads(space_out) + back[0]).astype(jnp.bfloat16)
    query_grad = (join_heads(space_grads[0]) + back[1]).astype(jnp.bfloat16)
    key_grad = (join_heads(space_grads[1]) + back[2]).astype(jnp.bfloat16)
    value_grad = (join_heads(space_grads[2]) + back[3]).astype(jnp.bfloat16)
    return (attended, query_grad, key_grad, value_grad, bias_grad)


def solution(mesh):
    return jax.shard_map(
        on_device,
        mesh=mesh,
        in_specs=(
            P("dp", "seq", None, None),
            P("dp", "seq", None, None),
            P("dp", "seq", None, None),
            P("dp", "seq", None, None),
            P("dp", "seq"),
            P("dp", None),
            P(),
        ),
        out_specs=(
            P("dp", "seq", None, None),
            P("dp", "seq", None, None),
            P("dp", "seq", None, None),
            P("dp", "seq", None, None),
            P(),
        ),
        check_vma=False,
    )
```

```python
import math

import jax
import jax.numpy as jnp
from jax import lax
from jax.sharding import PartitionSpec as P

SPACE_PATTERNS = ("bfihe,bfjhe->bfhij", "bfhij,bfjhe->bfihe", "bfhij,bfihe->bfjhe")
TIME_PATTERNS = ("biphe,bjphe->bphij", "bphij,bjphe->biphe", "bphij,biphe->bjphe")


def split_heads(tensor, head_count):
    return tensor.reshape(tensor.shape[:-1] + (head_count, tensor.shape[-1] // head_count))


def join_heads(tensor):
    return tensor.reshape(tensor.shape[:-2] + (tensor.shape[-2] * tensor.shape[-1],))


def attend_forward(patterns, query_part, key_part, value_part, bias, allowed):
    scaling = 1.0 / math.sqrt(query_part.shape[-1])
    scores = (
        jnp.einsum(patterns[0], query_part, key_part, preferred_element_type=jnp.float32) * scaling
        + bias
    )
    scores = jnp.where(allowed, scores, -1e30)
    row_peak = jnp.max(scores, axis=-1, keepdims=True)
    weights = jnp.exp(scores - row_peak)
    shares = weights / jnp.sum(weights, axis=-1, keepdims=True)
    shares_half = shares.astype(jnp.bfloat16)
    result = jnp.einsum(patterns[1], shares_half, value_part, preferred_element_type=jnp.float32)
    return (shares, shares_half, result)


def attend_backward(
    patterns, query_part, key_part, value_part, cotangent_part, shares, shares_half
):
    scaling = 1.0 / math.sqrt(query_part.shape[-1])
    value_grad = jnp.einsum(
        patterns[2], shares_half, cotangent_part, preferred_element_type=jnp.float32
    )
    share_grad = jnp.einsum(
        patterns[0], cotangent_part, value_part, preferred_element_type=jnp.float32
    )
    spread = jnp.sum(shares * share_grad, axis=-1, keepdims=True)
    score_grad = shares * (share_grad - spread)
    score_half = score_grad.astype(jnp.bfloat16)
    query_grad = (
        jnp.einsum(patterns[1], score_half, key_part, preferred_element_type=jnp.float32) * scaling
    )
    key_grad = (
        jnp.einsum(patterns[2], score_half, query_part, preferred_element_type=jnp.float32)
        * scaling
    )
    return (query_grad, key_grad, value_grad, score_grad)


def quad_sum(value, axis, size):
    step = 1
    while step < size:
        received = [
            lax.ppermute(value, axis, [(index, index ^ (part * step)) for index in range(size)])
            for part in (1, 2, 3)
        ]
        value = (value + received[0]) + (received[1] + received[2])
        step *= 4
    return value


def on_device(queries, keys, values, cotangent, spatial_count, clip_ids, time_bias):
    head_count, frames_all = time_bias.shape
    positions = queries.shape[2]
    width = queries.shape[3]
    seq_size = lax.axis_size("seq")
    dp_size = lax.axis_size("dp")
    row_index = lax.broadcasted_iota(jnp.int32, (frames_all, frames_all), 0)
    col_index = lax.broadcasted_iota(jnp.int32, (frames_all, frames_all), 1)
    distance = jnp.abs(row_index - col_index)
    lag_index = lax.broadcasted_iota(jnp.int32, (frames_all, frames_all, frames_all), 0)
    onehot = (lag_index == distance[None]).astype(jnp.float32)
    bias_table = jnp.tensordot(time_bias, onehot, axes=1, precision=lax.Precision.HIGHEST)[
        None, None
    ]
    same_clip = (clip_ids[:, :, None] == clip_ids[:, None, :])[:, None, None]
    position = lax.broadcasted_iota(jnp.int32, (1, 1, 1, 1, positions), 4)
    live_keys = position < spatial_count[:, :, None, None, None]

    block = positions // seq_size
    stacked = jnp.stack([queries[0, 0], keys[0, 0], values[0, 0], cotangent[0, 0]])
    stacked = stacked.reshape(4, seq_size, block, width)
    rows = lax.all_to_all(stacked, "seq", split_axis=1, concat_axis=1, tiled=True)
    query_part = split_heads(rows[0][None], head_count)
    key_part = split_heads(rows[1][None], head_count)
    value_part = split_heads(rows[2][None], head_count)
    slope_part = split_heads(rows[3][None], head_count)
    shares, shares_half, result = attend_forward(
        TIME_PATTERNS, query_part, key_part, value_part, bias_table, same_clip
    )
    time_grads = attend_backward(
        TIME_PATTERNS, query_part, key_part, value_part, slope_part, shares, shares_half
    )
    bias_part = jnp.tensordot(
        jnp.sum(time_grads[3], axis=(0, 1)),
        onehot,
        axes=((1, 2), (1, 2)),
        precision=lax.Precision.HIGHEST,
    )
    summed = quad_sum(quad_sum(bias_part, "seq", seq_size), "dp", dp_size)
    bias_grad = summed / math.sqrt(dp_size * queries.shape[0] * frames_all * positions)

    back_rows = jnp.stack(
        [
            join_heads(result[0]).astype(jnp.bfloat16),
            join_heads(time_grads[0][0]).astype(jnp.bfloat16),
            join_heads(time_grads[1][0]).astype(jnp.bfloat16),
            join_heads(time_grads[2][0]).astype(jnp.bfloat16),
        ]
    )
    back = lax.all_to_all(back_rows, "seq", split_axis=1, concat_axis=2, tiled=True)
    back = back.reshape(4, 1, 1, positions, width).astype(jnp.float32)

    space_query = split_heads(queries, head_count)
    space_key = split_heads(keys, head_count)
    space_value = split_heads(values, head_count)
    space_slope = split_heads(cotangent, head_count)
    space_shares, space_half, space_out = attend_forward(
        SPACE_PATTERNS, space_query, space_key, space_value, 0.0, live_keys
    )
    space_grads = attend_backward(
        SPACE_PATTERNS, space_query, space_key, space_value, space_slope, space_shares, space_half
    )
    attended = (join_heads(space_out) + back[0]).astype(jnp.bfloat16)
    query_grad = (join_heads(space_grads[0]) + back[1]).astype(jnp.bfloat16)
    key_grad = (join_heads(space_grads[1]) + back[2]).astype(jnp.bfloat16)
    value_grad = (join_heads(space_grads[2]) + back[3]).astype(jnp.bfloat16)
    return (attended, query_grad, key_grad, value_grad, bias_grad)


def solution(mesh):
    return jax.shard_map(
        on_device,
        mesh=mesh,
        in_specs=(
            P("dp", "seq", None, None),
            P("dp", "seq", None, None),
            P("dp", "seq", None, None),
            P("dp", "seq", None, None),
            P("dp", "seq"),
            P("dp", None),
            P(),
        ),
        out_specs=(
            P("dp", "seq", None, None),
            P("dp", "seq", None, None),
            P("dp", "seq", None, None),
            P("dp", "seq", None, None),
            P(),
        ),
        check_vma=False,
    )
```

```python
import math

import jax
import jax.numpy as jnp
from jax import lax
from jax.sharding import PartitionSpec as P

SPACE_PATTERNS = ("bfihe,bfjhe->bfhij", "bfhij,bfjhe->bfihe", "bfhij,bfihe->bfjhe")
TIME_PATTERNS = ("phie,phje->phij", "phij,phje->phie", "phij,phie->phje")


def split_heads(tensor, head_count):
    return tensor.reshape(tensor.shape[:-1] + (head_count, tensor.shape[-1] // head_count))


def join_heads(tensor):
    return tensor.reshape(tensor.shape[:-2] + (tensor.shape[-2] * tensor.shape[-1],))


def attend_forward(patterns, query_part, key_part, value_part, bias, allowed):
    scaling = 1.0 / math.sqrt(query_part.shape[-1])
    scores = (
        jnp.einsum(patterns[0], query_part, key_part, preferred_element_type=jnp.float32) * scaling
        + bias
    )
    scores = jnp.where(allowed, scores, -1e30)
    row_peak = jnp.max(scores, axis=-1, keepdims=True)
    weights = jnp.exp(scores - row_peak)
    shares = weights / jnp.sum(weights, axis=-1, keepdims=True)
    shares_half = shares.astype(jnp.bfloat16)
    result = jnp.einsum(patterns[1], shares_half, value_part, preferred_element_type=jnp.float32)
    return (shares, shares_half, result)


def attend_backward(
    patterns, query_part, key_part, value_part, cotangent_part, shares, shares_half
):
    scaling = 1.0 / math.sqrt(query_part.shape[-1])
    value_grad = jnp.einsum(
        patterns[2], shares_half, cotangent_part, preferred_element_type=jnp.float32
    )
    share_grad = jnp.einsum(
        patterns[0], cotangent_part, value_part, preferred_element_type=jnp.float32
    )
    spread = jnp.sum(shares * share_grad, axis=-1, keepdims=True)
    score_grad = shares * (share_grad - spread)
    score_half = score_grad.astype(jnp.bfloat16)
    query_grad = (
        jnp.einsum(patterns[1], score_half, key_part, preferred_element_type=jnp.float32) * scaling
    )
    key_grad = (
        jnp.einsum(patterns[2], score_half, query_part, preferred_element_type=jnp.float32)
        * scaling
    )
    return (query_grad, key_grad, value_grad, score_grad)


def quad_sum(value, axis, size):
    step = 1
    while step < size:
        received = [
            lax.ppermute(value, axis, [(index, index ^ (part * step)) for index in range(size)])
            for part in (1, 2, 3)
        ]
        value = (value + received[0]) + (received[1] + received[2])
        step *= 4
    return value


def on_device(queries, keys, values, cotangent, spatial_count, clip_ids, time_bias):
    head_count, frames_all = time_bias.shape
    positions = queries.shape[2]
    width = queries.shape[3]
    seq_size = lax.axis_size("seq")
    dp_size = lax.axis_size("dp")
    row_index = lax.broadcasted_iota(jnp.int32, (frames_all, frames_all), 0)
    col_index = lax.broadcasted_iota(jnp.int32, (frames_all, frames_all), 1)
    distance = jnp.abs(row_index - col_index)
    lag_index = lax.broadcasted_iota(jnp.int32, (frames_all, frames_all, frames_all), 0)
    onehot = (lag_index == distance[None]).astype(jnp.float32)
    bias_table = jnp.tensordot(time_bias, onehot, axes=1, precision=lax.Precision.HIGHEST)[
        None, None
    ]
    same_clip = (clip_ids[:, :, None] == clip_ids[:, None, :])[:, None, None]
    position = lax.broadcasted_iota(jnp.int32, (1, 1, 1, 1, positions), 4)
    live_keys = position < spatial_count[:, :, None, None, None]

    block = positions // seq_size
    stacked = jnp.stack(
        [
            tensor.reshape(seq_size, block, width)
            for tensor in (queries, keys, values, cotangent)
        ],
        axis=2,
    )
    rows = lax.all_to_all(stacked, "seq", split_axis=0, concat_axis=0, tiled=True)
    rows = rows.reshape(seq_size, block, 4, head_count, width // head_count)
    rows = jnp.transpose(rows, (2, 1, 3, 0, 4))
    query_part, key_part, value_part, slope_part = rows[0], rows[1], rows[2], rows[3]
    shares, shares_half, result = attend_forward(
        TIME_PATTERNS, query_part, key_part, value_part, bias_table[0], same_clip[0]
    )
    time_grads = attend_backward(
        TIME_PATTERNS, query_part, key_part, value_part, slope_part, shares, shares_half
    )
    bias_part = jnp.tensordot(
        jnp.sum(time_grads[3], axis=0),
        onehot,
        axes=((1, 2), (1, 2)),
        precision=lax.Precision.HIGHEST,
    )
    summed = quad_sum(quad_sum(bias_part, "seq", seq_size), "dp", dp_size)
    bias_grad = summed / math.sqrt(dp_size * queries.shape[0] * frames_all * positions)

    back_rows = jnp.stack(
        [
            jnp.transpose(tensor.astype(jnp.bfloat16), (2, 0, 1, 3)).reshape(seq_size, block, width)
            for tensor in (result, time_grads[0], time_grads[1], time_grads[2])
        ],
        axis=2,
    )
    back = lax.all_to_all(back_rows, "seq", split_axis=0, concat_axis=0, tiled=True)
    back = jnp.moveaxis(back, 2, 0).reshape(4, 1, 1, positions, width).astype(jnp.float32)

    space_query = split_heads(queries, head_count)
    space_key = split_heads(keys, head_count)
    space_value = split_heads(values, head_count)
    space_slope = split_heads(cotangent, head_count)
    space_shares, space_half, space_out = attend_forward(
        SPACE_PATTERNS, space_query, space_key, space_value, 0.0, live_keys
    )
    space_grads = attend_backward(
        SPACE_PATTERNS, space_query, space_key, space_value, space_slope, space_shares, space_half
    )
    attended = (join_heads(space_out) + back[0]).astype(jnp.bfloat16)
    query_grad = (join_heads(space_grads[0]) + back[1]).astype(jnp.bfloat16)
    key_grad = (join_heads(space_grads[1]) + back[2]).astype(jnp.bfloat16)
    value_grad = (join_heads(space_grads[2]) + back[3]).astype(jnp.bfloat16)
    return (attended, query_grad, key_grad, value_grad, bias_grad)


def solution(mesh):
    return jax.shard_map(
        on_device,
        mesh=mesh,
        in_specs=(
            P("dp", "seq", None, None),
            P("dp", "seq", None, None),
            P("dp", "seq", None, None),
            P("dp", "seq", None, None),
            P("dp", "seq"),
            P("dp", None),
            P(),
        ),
        out_specs=(
            P("dp", "seq", None, None),
            P("dp", "seq", None, None),
            P("dp", "seq", None, None),
            P("dp", "seq", None, None),
            P(),
        ),
        check_vma=False,
    )
```

```python
import math

import jax
import jax.numpy as jnp
from jax import lax
from jax.sharding import PartitionSpec as P

SPACE_PATTERNS = ("bfihe,bfjhe->bfhij", "bfhij,bfjhe->bfihe", "bfhij,bfihe->bfjhe")
TIME_PATTERNS = ("phie,phje->phij", "phij,phje->phie", "phij,phie->phje")


def split_heads(tensor, head_count):
    return tensor.reshape(tensor.shape[:-1] + (head_count, tensor.shape[-1] // head_count))


def join_heads(tensor):
    return tensor.reshape(tensor.shape[:-2] + (tensor.shape[-2] * tensor.shape[-1],))


def attend_forward(patterns, query_part, key_part, value_part, bias, allowed):
    scaling = 1.0 / math.sqrt(query_part.shape[-1])
    scores = (
        jnp.einsum(patterns[0], query_part, key_part, preferred_element_type=jnp.float32) * scaling
        + bias
    )
    scores = jnp.where(allowed, scores, -1e30)
    row_peak = jnp.max(scores, axis=-1, keepdims=True)
    weights = jnp.exp(scores - row_peak)
    shares = weights / jnp.sum(weights, axis=-1, keepdims=True)
    shares_half = shares.astype(jnp.bfloat16)
    result = jnp.einsum(patterns[1], shares_half, value_part, preferred_element_type=jnp.float32)
    return (shares, shares_half, result)


def attend_backward(
    patterns, query_part, key_part, value_part, cotangent_part, shares, shares_half
):
    scaling = 1.0 / math.sqrt(query_part.shape[-1])
    value_grad = jnp.einsum(
        patterns[2], shares_half, cotangent_part, preferred_element_type=jnp.float32
    )
    share_grad = jnp.einsum(
        patterns[0], cotangent_part, value_part, preferred_element_type=jnp.float32
    )
    spread = jnp.sum(shares * share_grad, axis=-1, keepdims=True)
    score_grad = shares * (share_grad - spread)
    score_half = score_grad.astype(jnp.bfloat16)
    query_grad = (
        jnp.einsum(patterns[1], score_half, key_part, preferred_element_type=jnp.float32) * scaling
    )
    key_grad = (
        jnp.einsum(patterns[2], score_half, query_part, preferred_element_type=jnp.float32)
        * scaling
    )
    return (query_grad, key_grad, value_grad, score_grad)


def quad_step(value, axis, size, step):
    received = [
        lax.ppermute(value, axis, [(index, index ^ (part * step)) for index in range(size)])
        for part in (1, 2, 3)
    ]
    return (value + received[0]) + (received[1] + received[2])


def on_device(queries, keys, values, cotangent, spatial_count, clip_ids, time_bias):
    head_count, frames_all = time_bias.shape
    positions = queries.shape[2]
    width = queries.shape[3]
    seq_size = lax.axis_size("seq")
    dp_size = lax.axis_size("dp")
    row_index = lax.broadcasted_iota(jnp.int32, (frames_all, frames_all), 0)
    col_index = lax.broadcasted_iota(jnp.int32, (frames_all, frames_all), 1)
    distance = jnp.abs(row_index - col_index)
    lag_index = lax.broadcasted_iota(jnp.int32, (frames_all, frames_all, frames_all), 0)
    onehot = (lag_index == distance[None]).astype(jnp.float32)
    bias_table = jnp.tensordot(time_bias, onehot, axes=1, precision=lax.Precision.HIGHEST)[
        None, None
    ]
    same_clip = (clip_ids[:, :, None] == clip_ids[:, None, :])[:, None, None]
    position = lax.broadcasted_iota(jnp.int32, (1, 1, 1, 1, positions), 4)
    live_keys = position < spatial_count[:, :, None, None, None]

    block = positions // seq_size
    stacked = jnp.stack(
        [
            tensor.reshape(seq_size, block, width)
            for tensor in (queries, keys, values, cotangent)
        ],
        axis=2,
    )
    rows = lax.all_to_all(stacked, "seq", split_axis=0, concat_axis=0, tiled=True)
    rows = rows.reshape(seq_size, block, 4, head_count, width // head_count)
    rows = jnp.transpose(rows, (2, 1, 3, 0, 4))
    query_part, key_part, value_part, slope_part = rows[0], rows[1], rows[2], rows[3]
    scaling = 1.0 / math.sqrt(query_part.shape[-1])
    scores = (
        jnp.einsum(TIME_PATTERNS[0], query_part, key_part, preferred_element_type=jnp.float32)
        * scaling
        + bias_table[0]
    )
    scores = jnp.where(same_clip[0], scores, -1e30)
    row_peak = jnp.max(scores, axis=-1, keepdims=True)
    weights = jnp.exp(scores - row_peak)
    shares = weights / jnp.sum(weights, axis=-1, keepdims=True)
    share_grad = jnp.einsum(
        TIME_PATTERNS[0], slope_part, value_part, preferred_element_type=jnp.float32
    )
    spread = jnp.sum(shares * share_grad, axis=-1, keepdims=True)
    score_grad = shares * (share_grad - spread)
    bias_part = jnp.tensordot(
        jnp.sum(score_grad, axis=0),
        onehot,
        axes=((1, 2), (1, 2)),
        precision=lax.Precision.HIGHEST,
    )
    partial = quad_step(bias_part, "seq", seq_size, 1)
    partial, shares, score_grad, query_part, key_part, value_part, slope_part = (
        lax.optimization_barrier(
            (partial, shares, score_grad, query_part, key_part, value_part, slope_part)
        )
    )
    shares_half = shares.astype(jnp.bfloat16)
    score_half = score_grad.astype(jnp.bfloat16)
    result = jnp.einsum(
        TIME_PATTERNS[1], shares_half, value_part, preferred_element_type=jnp.float32
    )
    time_value_grad = jnp.einsum(
        TIME_PATTERNS[2], shares_half, slope_part, preferred_element_type=jnp.float32
    )
    time_query_grad = (
        jnp.einsum(TIME_PATTERNS[1], score_half, key_part, preferred_element_type=jnp.float32)
        * scaling
    )
    time_key_grad = (
        jnp.einsum(TIME_PATTERNS[2], score_half, query_part, preferred_element_type=jnp.float32)
        * scaling
    )
    partial = quad_step(partial, "seq", seq_size, 4)
    back_rows = jnp.stack(
        [
            jnp.transpose(tensor.astype(jnp.bfloat16), (2, 0, 1, 3)).reshape(seq_size, block, width)
            for tensor in (result, time_query_grad, time_key_grad, time_value_grad)
        ],
        axis=2,
    )
    partial, back_rows = lax.optimization_barrier((partial, back_rows))
    summed = quad_step(quad_step(partial, "dp", dp_size, 1), "dp", dp_size, 4)
    bias_grad = summed / math.sqrt(dp_size * queries.shape[0] * frames_all * positions)
    back = lax.all_to_all(back_rows, "seq", split_axis=0, concat_axis=0, tiled=True)
    back = jnp.moveaxis(back, 2, 0).reshape(4, 1, 1, positions, width).astype(jnp.float32)

    space_query = split_heads(queries, head_count)
    space_key = split_heads(keys, head_count)
    space_value = split_heads(values, head_count)
    space_slope = split_heads(cotangent, head_count)
    space_shares, space_half, space_out = attend_forward(
        SPACE_PATTERNS, space_query, space_key, space_value, 0.0, live_keys
    )
    space_grads = attend_backward(
        SPACE_PATTERNS, space_query, space_key, space_value, space_slope, space_shares, space_half
    )
    attended = (join_heads(space_out) + back[0]).astype(jnp.bfloat16)
    query_grad = (join_heads(space_grads[0]) + back[1]).astype(jnp.bfloat16)
    key_grad = (join_heads(space_grads[1]) + back[2]).astype(jnp.bfloat16)
    value_grad = (join_heads(space_grads[2]) + back[3]).astype(jnp.bfloat16)
    return (attended, query_grad, key_grad, value_grad, bias_grad)


def solution(mesh):
    return jax.shard_map(
        on_device,
        mesh=mesh,
        in_specs=(
            P("dp", "seq", None, None),
            P("dp", "seq", None, None),
            P("dp", "seq", None, None),
            P("dp", "seq", None, None),
            P("dp", "seq"),
            P("dp", None),
            P(),
        ),
        out_specs=(
            P("dp", "seq", None, None),
            P("dp", "seq", None, None),
            P("dp", "seq", None, None),
            P("dp", "seq", None, None),
            P(),
        ),
        check_vma=False,
    )
```

```python
import math

import jax
import jax.numpy as jnp
from jax import lax
from jax.sharding import PartitionSpec as P

SPACE_PATTERNS = ("bfihe,bfjhe->bfhij", "bfhij,bfjhe->bfihe", "bfhij,bfihe->bfjhe")
TIME_PATTERNS = ("phie,phje->phij", "phij,phje->phie", "phij,phie->phje")


def split_heads(tensor, head_count):
    return tensor.reshape(tensor.shape[:-1] + (head_count, tensor.shape[-1] // head_count))


def join_heads(tensor):
    return tensor.reshape(tensor.shape[:-2] + (tensor.shape[-2] * tensor.shape[-1],))


def attend_forward(patterns, query_part, key_part, value_part, bias, allowed):
    scaling = 1.0 / math.sqrt(query_part.shape[-1])
    scores = (
        jnp.einsum(patterns[0], query_part, key_part, preferred_element_type=jnp.float32) * scaling
        + bias
    )
    scores = jnp.where(allowed, scores, -1e30)
    row_peak = jnp.max(scores, axis=-1, keepdims=True)
    weights = jnp.exp(scores - row_peak)
    shares = weights / jnp.sum(weights, axis=-1, keepdims=True)
    shares_half = shares.astype(jnp.bfloat16)
    result = jnp.einsum(patterns[1], shares_half, value_part, preferred_element_type=jnp.float32)
    return (shares, shares_half, result)


def attend_backward(
    patterns, query_part, key_part, value_part, cotangent_part, shares, shares_half
):
    scaling = 1.0 / math.sqrt(query_part.shape[-1])
    value_grad = jnp.einsum(
        patterns[2], shares_half, cotangent_part, preferred_element_type=jnp.float32
    )
    share_grad = jnp.einsum(
        patterns[0], cotangent_part, value_part, preferred_element_type=jnp.float32
    )
    spread = jnp.sum(shares * share_grad, axis=-1, keepdims=True)
    score_grad = shares * (share_grad - spread)
    score_half = score_grad.astype(jnp.bfloat16)
    query_grad = (
        jnp.einsum(patterns[1], score_half, key_part, preferred_element_type=jnp.float32) * scaling
    )
    key_grad = (
        jnp.einsum(patterns[2], score_half, query_part, preferred_element_type=jnp.float32)
        * scaling
    )
    return (query_grad, key_grad, value_grad, score_grad)


def quad_step(value, axis, size, step):
    received = [
        lax.ppermute(value, axis, [(index, index ^ (part * step)) for index in range(size)])
        for part in (1, 2, 3)
    ]
    return (value + received[0]) + (received[1] + received[2])


def on_device(queries, keys, values, cotangent, spatial_count, clip_ids, time_bias):
    head_count, frames_all = time_bias.shape
    positions = queries.shape[2]
    width = queries.shape[3]
    seq_size = lax.axis_size("seq")
    dp_size = lax.axis_size("dp")
    row_index = lax.broadcasted_iota(jnp.int32, (frames_all, frames_all), 0)
    col_index = lax.broadcasted_iota(jnp.int32, (frames_all, frames_all), 1)
    distance = jnp.abs(row_index - col_index)
    lag_index = lax.broadcasted_iota(jnp.int32, (frames_all, frames_all, frames_all), 0)
    onehot = (lag_index == distance[None]).astype(jnp.float32)
    bias_table = jnp.tensordot(time_bias, onehot, axes=1, precision=lax.Precision.HIGHEST)[
        None, None
    ]
    same_clip = (clip_ids[:, :, None] == clip_ids[:, None, :])[:, None, None]
    position = lax.broadcasted_iota(jnp.int32, (1, 1, 1, 1, positions), 4)
    live_keys = position < spatial_count[:, :, None, None, None]

    block = positions // seq_size
    stacked = jnp.stack(
        [
            tensor.reshape(seq_size, block, width)
            for tensor in (queries, keys, values, cotangent)
        ],
        axis=2,
    )
    rows = lax.all_to_all(stacked, "seq", split_axis=0, concat_axis=0, tiled=True)
    rows = rows.reshape(seq_size, block, 4, head_count, width // head_count)
    rows = jnp.transpose(rows, (2, 1, 3, 0, 4))
    query_part, key_part, value_part, slope_part = rows[0], rows[1], rows[2], rows[3]
    scaling = 1.0 / math.sqrt(query_part.shape[-1])
    scores = (
        jnp.einsum(TIME_PATTERNS[0], query_part, key_part, preferred_element_type=jnp.float32)
        * scaling
        + bias_table[0]
    )
    scores = jnp.where(same_clip[0], scores, -1e30)
    row_peak = jnp.max(scores, axis=-1, keepdims=True)
    weights = jnp.exp(scores - row_peak)
    shares = weights / jnp.sum(weights, axis=-1, keepdims=True)
    share_grad = jnp.einsum(
        TIME_PATTERNS[0], slope_part, value_part, preferred_element_type=jnp.float32
    )
    spread = jnp.sum(shares * share_grad, axis=-1, keepdims=True)
    score_grad = shares * (share_grad - spread)
    bias_part = jnp.tensordot(
        jnp.sum(score_grad, axis=0),
        onehot,
        axes=((1, 2), (1, 2)),
        precision=lax.Precision.HIGHEST,
    )
    partial = quad_step(bias_part, "seq", seq_size, 1)
    shares_half = shares.astype(jnp.bfloat16)
    score_half = score_grad.astype(jnp.bfloat16)
    result = jnp.einsum(
        TIME_PATTERNS[1], shares_half, value_part, preferred_element_type=jnp.float32
    )
    time_value_grad = jnp.einsum(
        TIME_PATTERNS[2], shares_half, slope_part, preferred_element_type=jnp.float32
    )
    time_query_grad = (
        jnp.einsum(TIME_PATTERNS[1], score_half, key_part, preferred_element_type=jnp.float32)
        * scaling
    )
    time_key_grad = (
        jnp.einsum(TIME_PATTERNS[2], score_half, query_part, preferred_element_type=jnp.float32)
        * scaling
    )
    partial = quad_step(partial, "seq", seq_size, 4)
    back_rows = jnp.stack(
        [
            jnp.transpose(tensor.astype(jnp.bfloat16), (2, 0, 1, 3)).reshape(seq_size, block, width)
            for tensor in (result, time_query_grad, time_key_grad, time_value_grad)
        ],
        axis=2,
    )
    partial, back_rows = lax.optimization_barrier((partial, back_rows))
    summed = quad_step(quad_step(partial, "dp", dp_size, 1), "dp", dp_size, 4)
    bias_grad = summed / math.sqrt(dp_size * queries.shape[0] * frames_all * positions)
    back = lax.all_to_all(back_rows, "seq", split_axis=0, concat_axis=0, tiled=True)
    back = jnp.moveaxis(back, 2, 0).reshape(4, 1, 1, positions, width).astype(jnp.float32)

    space_query = split_heads(queries, head_count)
    space_key = split_heads(keys, head_count)
    space_value = split_heads(values, head_count)
    space_slope = split_heads(cotangent, head_count)
    space_shares, space_half, space_out = attend_forward(
        SPACE_PATTERNS, space_query, space_key, space_value, 0.0, live_keys
    )
    space_grads = attend_backward(
        SPACE_PATTERNS, space_query, space_key, space_value, space_slope, space_shares, space_half
    )
    attended = (join_heads(space_out) + back[0]).astype(jnp.bfloat16)
    query_grad = (join_heads(space_grads[0]) + back[1]).astype(jnp.bfloat16)
    key_grad = (join_heads(space_grads[1]) + back[2]).astype(jnp.bfloat16)
    value_grad = (join_heads(space_grads[2]) + back[3]).astype(jnp.bfloat16)
    return (attended, query_grad, key_grad, value_grad, bias_grad)


def solution(mesh):
    return jax.shard_map(
        on_device,
        mesh=mesh,
        in_specs=(
            P("dp", "seq", None, None),
            P("dp", "seq", None, None),
            P("dp", "seq", None, None),
            P("dp", "seq", None, None),
            P("dp", "seq"),
            P("dp", None),
            P(),
        ),
        out_specs=(
            P("dp", "seq", None, None),
            P("dp", "seq", None, None),
            P("dp", "seq", None, None),
            P("dp", "seq", None, None),
            P(),
        ),
        check_vma=False,
    )
```

```python
import math

import jax
import jax.numpy as jnp
from jax import lax
from jax.sharding import PartitionSpec as P
from jax.experimental import pallas as pl

SPACE_PATTERNS = ("bfihe,bfjhe->bfhij", "bfhij,bfjhe->bfihe", "bfhij,bfihe->bfjhe")
TIME_PATTERNS = ("phie,phje->phij", "phij,phje->phie", "phij,phie->phje")


def split_heads(tensor, head_count):
    return tensor.reshape(tensor.shape[:-1] + (head_count, tensor.shape[-1] // head_count))


def join_heads(tensor):
    return tensor.reshape(tensor.shape[:-2] + (tensor.shape[-2] * tensor.shape[-1],))


def attend_forward(patterns, query_part, key_part, value_part, bias, allowed):
    scaling = 1.0 / math.sqrt(query_part.shape[-1])
    scores = (
        jnp.einsum(patterns[0], query_part, key_part, preferred_element_type=jnp.float32) * scaling
        + bias
    )
    scores = jnp.where(allowed, scores, -1e30)
    row_peak = jnp.max(scores, axis=-1, keepdims=True)
    weights = jnp.exp(scores - row_peak)
    shares = weights / jnp.sum(weights, axis=-1, keepdims=True)
    shares_half = shares.astype(jnp.bfloat16)
    result = jnp.einsum(patterns[1], shares_half, value_part, preferred_element_type=jnp.float32)
    return (shares, shares_half, result)


def attend_backward(
    patterns, query_part, key_part, value_part, cotangent_part, shares, shares_half
):
    scaling = 1.0 / math.sqrt(query_part.shape[-1])
    value_grad = jnp.einsum(
        patterns[2], shares_half, cotangent_part, preferred_element_type=jnp.float32
    )
    share_grad = jnp.einsum(
        patterns[0], cotangent_part, value_part, preferred_element_type=jnp.float32
    )
    spread = jnp.sum(shares * share_grad, axis=-1, keepdims=True)
    score_grad = shares * (share_grad - spread)
    score_half = score_grad.astype(jnp.bfloat16)
    query_grad = (
        jnp.einsum(patterns[1], score_half, key_part, preferred_element_type=jnp.float32) * scaling
    )
    key_grad = (
        jnp.einsum(patterns[2], score_half, query_part, preferred_element_type=jnp.float32)
        * scaling
    )
    return (query_grad, key_grad, value_grad, score_grad)


def regroup_kernel(x_ref, o_ref):
    frames, block, tensors, width = x_ref.shape
    heads, size = o_ref.shape[2], o_ref.shape[4]
    for tensor in range(tensors):
        for place in range(block):
            row = x_ref[:, place, tensor, :]
            for head in range(heads):
                o_ref[tensor, place, head] = row[:, head * size : (head + 1) * size]


def regroup(rows, heads):
    frames, block, tensors, width = rows.shape
    size = width // heads
    return pl.pallas_call(
        regroup_kernel,
        out_shape=jax.ShapeDtypeStruct((tensors, block, heads, frames, size), rows.dtype),
    )(rows)


def quad_step(value, axis, size, step):
    received = [
        lax.ppermute(value, axis, [(index, index ^ (part * step)) for index in range(size)])
        for part in (1, 2, 3)
    ]
    return (value + received[0]) + (received[1] + received[2])


def on_device(queries, keys, values, cotangent, spatial_count, clip_ids, time_bias):
    head_count, frames_all = time_bias.shape
    positions = queries.shape[2]
    width = queries.shape[3]
    seq_size = lax.axis_size("seq")
    dp_size = lax.axis_size("dp")
    row_index = lax.broadcasted_iota(jnp.int32, (frames_all, frames_all), 0)
    col_index = lax.broadcasted_iota(jnp.int32, (frames_all, frames_all), 1)
    distance = jnp.abs(row_index - col_index)
    lag_index = lax.broadcasted_iota(jnp.int32, (frames_all, frames_all, frames_all), 0)
    onehot = (lag_index == distance[None]).astype(jnp.float32)
    bias_table = jnp.tensordot(time_bias, onehot, axes=1, precision=lax.Precision.HIGHEST)[
        None, None
    ]
    same_clip = (clip_ids[:, :, None] == clip_ids[:, None, :])[:, None, None]
    position = lax.broadcasted_iota(jnp.int32, (1, 1, 1, 1, positions), 4)
    live_keys = position < spatial_count[:, :, None, None, None]

    block = positions // seq_size
    stacked = jnp.stack(
        [
            tensor.reshape(seq_size, block, width)
            for tensor in (queries, keys, values, cotangent)
        ],
        axis=2,
    )
    rows = lax.all_to_all(stacked, "seq", split_axis=0, concat_axis=0, tiled=True)
    rows = regroup(rows, head_count)
    query_part, key_part, value_part, slope_part = rows[0], rows[1], rows[2], rows[3]
    scaling = 1.0 / math.sqrt(query_part.shape[-1])
    scores = (
        jnp.einsum(TIME_PATTERNS[0], query_part, key_part, preferred_element_type=jnp.float32)
        * scaling
        + bias_table[0]
    )
    scores = jnp.where(same_clip[0], scores, -1e30)
    row_peak = jnp.max(scores, axis=-1, keepdims=True)
    weights = jnp.exp(scores - row_peak)
    shares = weights / jnp.sum(weights, axis=-1, keepdims=True)
    share_grad = jnp.einsum(
        TIME_PATTERNS[0], slope_part, value_part, preferred_element_type=jnp.float32
    )
    spread = jnp.sum(shares * share_grad, axis=-1, keepdims=True)
    score_grad = shares * (share_grad - spread)
    bias_part = jnp.tensordot(
        jnp.sum(score_grad, axis=0),
        onehot,
        axes=((1, 2), (1, 2)),
        precision=lax.Precision.HIGHEST,
    )
    partial = quad_step(bias_part, "seq", seq_size, 1)
    partial, shares, score_grad, query_part, key_part, value_part, slope_part = (
        lax.optimization_barrier(
            (partial, shares, score_grad, query_part, key_part, value_part, slope_part)
        )
    )
    shares_half = shares.astype(jnp.bfloat16)
    score_half = score_grad.astype(jnp.bfloat16)
    result = jnp.einsum(
        TIME_PATTERNS[1], shares_half, value_part, preferred_element_type=jnp.float32
    )
    time_value_grad = jnp.einsum(
        TIME_PATTERNS[2], shares_half, slope_part, preferred_element_type=jnp.float32
    )
    time_query_grad = (
        jnp.einsum(TIME_PATTERNS[1], score_half, key_part, preferred_element_type=jnp.float32)
        * scaling
    )
    time_key_grad = (
        jnp.einsum(TIME_PATTERNS[2], score_half, query_part, preferred_element_type=jnp.float32)
        * scaling
    )
    partial = quad_step(partial, "seq", seq_size, 4)
    back_rows = jnp.stack(
        [
            jnp.transpose(tensor.astype(jnp.bfloat16), (2, 0, 1, 3)).reshape(seq_size, block, width)
            for tensor in (result, time_query_grad, time_key_grad, time_value_grad)
        ],
        axis=2,
    )
    partial, back_rows = lax.optimization_barrier((partial, back_rows))
    summed = quad_step(quad_step(partial, "dp", dp_size, 1), "dp", dp_size, 4)
    bias_grad = summed / math.sqrt(dp_size * queries.shape[0] * frames_all * positions)
    back = lax.all_to_all(back_rows, "seq", split_axis=0, concat_axis=0, tiled=True)
    back = jnp.moveaxis(back, 2, 0).reshape(4, 1, 1, positions, width).astype(jnp.float32)

    space_query = split_heads(queries, head_count)
    space_key = split_heads(keys, head_count)
    space_value = split_heads(values, head_count)
    space_slope = split_heads(cotangent, head_count)
    space_shares, space_half, space_out = attend_forward(
        SPACE_PATTERNS, space_query, space_key, space_value, 0.0, live_keys
    )
    space_grads = attend_backward(
        SPACE_PATTERNS, space_query, space_key, space_value, space_slope, space_shares, space_half
    )
    attended = (join_heads(space_out) + back[0]).astype(jnp.bfloat16)
    query_grad = (join_heads(space_grads[0]) + back[1]).astype(jnp.bfloat16)
    key_grad = (join_heads(space_grads[1]) + back[2]).astype(jnp.bfloat16)
    value_grad = (join_heads(space_grads[2]) + back[3]).astype(jnp.bfloat16)
    return (attended, query_grad, key_grad, value_grad, bias_grad)


def solution(mesh):
    return jax.shard_map(
        on_device,
        mesh=mesh,
        in_specs=(
            P("dp", "seq", None, None),
            P("dp", "seq", None, None),
            P("dp", "seq", None, None),
            P("dp", "seq", None, None),
            P("dp", "seq"),
            P("dp", None),
            P(),
        ),
        out_specs=(
            P("dp", "seq", None, None),
            P("dp", "seq", None, None),
            P("dp", "seq", None, None),
            P("dp", "seq", None, None),
            P(),
        ),
        check_vma=False,
    )
```

```python
import math

import jax
import jax.numpy as jnp
from jax import lax
from jax.sharding import PartitionSpec as P

SPACE_PATTERNS = ("bfihe,bfjhe->bfhij", "bfhij,bfjhe->bfihe", "bfhij,bfihe->bfjhe")
TIME_PATTERNS = ("phie,phje->phij", "phij,phje->phie", "phij,phie->phje")


def split_heads(tensor, head_count):
    return tensor.reshape(tensor.shape[:-1] + (head_count, tensor.shape[-1] // head_count))


def join_heads(tensor):
    return tensor.reshape(tensor.shape[:-2] + (tensor.shape[-2] * tensor.shape[-1],))


def attend_forward(patterns, query_part, key_part, value_part, bias, allowed):
    scaling = 1.0 / math.sqrt(query_part.shape[-1])
    scores = (
        jnp.einsum(patterns[0], query_part, key_part, preferred_element_type=jnp.float32) * scaling
        + bias
    )
    scores = jnp.where(allowed, scores, -1e30)
    row_peak = jnp.max(scores, axis=-1, keepdims=True)
    weights = jnp.exp(scores - row_peak)
    shares = weights / jnp.sum(weights, axis=-1, keepdims=True)
    shares_half = shares.astype(jnp.bfloat16)
    result = jnp.einsum(patterns[1], shares_half, value_part, preferred_element_type=jnp.float32)
    return (shares, shares_half, result)


def attend_backward(
    patterns, query_part, key_part, value_part, cotangent_part, shares, shares_half
):
    scaling = 1.0 / math.sqrt(query_part.shape[-1])
    value_grad = jnp.einsum(
        patterns[2], shares_half, cotangent_part, preferred_element_type=jnp.float32
    )
    share_grad = jnp.einsum(
        patterns[0], cotangent_part, value_part, preferred_element_type=jnp.float32
    )
    spread = jnp.sum(shares * share_grad, axis=-1, keepdims=True)
    score_grad = shares * (share_grad - spread)
    score_half = score_grad.astype(jnp.bfloat16)
    query_grad = (
        jnp.einsum(patterns[1], score_half, key_part, preferred_element_type=jnp.float32) * scaling
    )
    key_grad = (
        jnp.einsum(patterns[2], score_half, query_part, preferred_element_type=jnp.float32)
        * scaling
    )
    return (query_grad, key_grad, value_grad, score_grad)


def quad_step(value, axis, size, step):
    received = [
        lax.ppermute(value, axis, [(index, index ^ (part * step)) for index in range(size)])
        for part in (1, 2, 3)
    ]
    return (value + received[0]) + (received[1] + received[2])


def on_device(queries, keys, values, cotangent, spatial_count, clip_ids, time_bias):
    head_count, frames_all = time_bias.shape
    positions = queries.shape[2]
    width = queries.shape[3]
    seq_size = lax.axis_size("seq")
    dp_size = lax.axis_size("dp")
    row_index = lax.broadcasted_iota(jnp.int32, (frames_all, frames_all), 0)
    col_index = lax.broadcasted_iota(jnp.int32, (frames_all, frames_all), 1)
    distance = jnp.abs(row_index - col_index)
    lag_index = lax.broadcasted_iota(jnp.int32, (frames_all, frames_all, frames_all), 0)
    onehot = (lag_index == distance[None]).astype(jnp.float32)
    bias_table = jnp.tensordot(time_bias, onehot, axes=1, precision=lax.Precision.HIGHEST)[
        None, None
    ]
    same_clip = (clip_ids[:, :, None] == clip_ids[:, None, :])[:, None, None]
    position = lax.broadcasted_iota(jnp.int32, (1, 1, 1, 1, positions), 4)
    live_keys = position < spatial_count[:, :, None, None, None]

    block = positions // seq_size
    stacked = jnp.stack(
        [
            tensor.reshape(seq_size, block, width)
            for tensor in (queries, keys, values, cotangent)
        ],
        axis=2,
    )
    rows = lax.all_to_all(stacked, "seq", split_axis=0, concat_axis=0, tiled=True)
    rows = rows.reshape(seq_size, block, 4, head_count, width // head_count)
    rows = jnp.transpose(rows, (2, 1, 3, 0, 4))
    query_part, key_part, value_part, slope_part = rows[0], rows[1], rows[2], rows[3]
    scaling = 1.0 / math.sqrt(query_part.shape[-1])
    scores = (
        jnp.einsum(TIME_PATTERNS[0], query_part, key_part, preferred_element_type=jnp.float32)
        * scaling
        + bias_table[0]
    )
    scores = jnp.where(same_clip[0], scores, -1e30)
    row_peak = jnp.max(scores, axis=-1, keepdims=True)
    weights = jnp.exp(scores - row_peak)
    shares = weights / jnp.sum(weights, axis=-1, keepdims=True)
    share_grad = jnp.einsum(
        TIME_PATTERNS[0], slope_part, value_part, preferred_element_type=jnp.float32
    )
    spread = jnp.sum(shares * share_grad, axis=-1, keepdims=True)
    score_grad = shares * (share_grad - spread)
    bias_part = jnp.tensordot(
        jnp.sum(score_grad, axis=0),
        onehot,
        axes=((1, 2), (1, 2)),
        precision=lax.Precision.HIGHEST,
    )
    partial = quad_step(bias_part, "seq", seq_size, 1)
    shares_half = shares.astype(jnp.bfloat16)
    result = jnp.einsum(
        TIME_PATTERNS[1], shares_half, value_part, preferred_element_type=jnp.float32
    )
    time_value_grad = jnp.einsum(
        TIME_PATTERNS[2], shares_half, slope_part, preferred_element_type=jnp.float32
    )
    partial, result, time_value_grad, score_grad, query_part, key_part = (
        lax.optimization_barrier(
            (partial, result, time_value_grad, score_grad, query_part, key_part)
        )
    )
    score_half = score_grad.astype(jnp.bfloat16)
    time_query_grad = (
        jnp.einsum(TIME_PATTERNS[1], score_half, key_part, preferred_element_type=jnp.float32)
        * scaling
    )
    time_key_grad = (
        jnp.einsum(TIME_PATTERNS[2], score_half, query_part, preferred_element_type=jnp.float32)
        * scaling
    )
    partial = quad_step(partial, "seq", seq_size, 4)
    back_rows = jnp.stack(
        [
            jnp.transpose(tensor.astype(jnp.bfloat16), (2, 0, 1, 3)).reshape(seq_size, block, width)
            for tensor in (result, time_query_grad, time_key_grad, time_value_grad)
        ],
        axis=2,
    )
    partial, back_rows = lax.optimization_barrier((partial, back_rows))
    summed = quad_step(quad_step(partial, "dp", dp_size, 1), "dp", dp_size, 4)
    bias_grad = summed / math.sqrt(dp_size * queries.shape[0] * frames_all * positions)
    back = lax.all_to_all(back_rows, "seq", split_axis=0, concat_axis=0, tiled=True)
    back = jnp.moveaxis(back, 2, 0).reshape(4, 1, 1, positions, width).astype(jnp.float32)

    space_query = split_heads(queries, head_count)
    space_key = split_heads(keys, head_count)
    space_value = split_heads(values, head_count)
    space_slope = split_heads(cotangent, head_count)
    space_shares, space_half, space_out = attend_forward(
        SPACE_PATTERNS, space_query, space_key, space_value, 0.0, live_keys
    )
    space_grads = attend_backward(
        SPACE_PATTERNS, space_query, space_key, space_value, space_slope, space_shares, space_half
    )
    attended = (join_heads(space_out) + back[0]).astype(jnp.bfloat16)
    query_grad = (join_heads(space_grads[0]) + back[1]).astype(jnp.bfloat16)
    key_grad = (join_heads(space_grads[1]) + back[2]).astype(jnp.bfloat16)
    value_grad = (join_heads(space_grads[2]) + back[3]).astype(jnp.bfloat16)
    return (attended, query_grad, key_grad, value_grad, bias_grad)


def solution(mesh):
    return jax.shard_map(
        on_device,
        mesh=mesh,
        in_specs=(
            P("dp", "seq", None, None),
            P("dp", "seq", None, None),
            P("dp", "seq", None, None),
            P("dp", "seq", None, None),
            P("dp", "seq"),
            P("dp", None),
            P(),
        ),
        out_specs=(
            P("dp", "seq", None, None),
            P("dp", "seq", None, None),
            P("dp", "seq", None, None),
            P("dp", "seq", None, None),
            P(),
        ),
        check_vma=False,
    )
```

```python
import math

import jax
import jax.numpy as jnp
from jax import lax
from jax.sharding import PartitionSpec as P

SPACE_PATTERNS = ("bfihe,bfjhe->bfhij", "bfhij,bfjhe->bfihe", "bfhij,bfihe->bfjhe")
TIME_PATTERNS = ("phie,phje->phij", "phij,phje->phie", "phij,phie->phje")


def split_heads(tensor, head_count):
    return tensor.reshape(tensor.shape[:-1] + (head_count, tensor.shape[-1] // head_count))


def join_heads(tensor):
    return tensor.reshape(tensor.shape[:-2] + (tensor.shape[-2] * tensor.shape[-1],))


def attend_forward(patterns, query_part, key_part, value_part, bias, allowed):
    scaling = 1.0 / math.sqrt(query_part.shape[-1])
    scores = (
        jnp.einsum(patterns[0], query_part, key_part, preferred_element_type=jnp.float32) * scaling
        + bias
    )
    scores = jnp.where(allowed, scores, -1e30)
    row_peak = jnp.max(scores, axis=-1, keepdims=True)
    weights = jnp.exp(scores - row_peak)
    shares = weights / jnp.sum(weights, axis=-1, keepdims=True)
    shares_half = shares.astype(jnp.bfloat16)
    result = jnp.einsum(patterns[1], shares_half, value_part, preferred_element_type=jnp.float32)
    return (shares, shares_half, result)


def attend_backward(
    patterns, query_part, key_part, value_part, cotangent_part, shares, shares_half
):
    scaling = 1.0 / math.sqrt(query_part.shape[-1])
    value_grad = jnp.einsum(
        patterns[2], shares_half, cotangent_part, preferred_element_type=jnp.float32
    )
    share_grad = jnp.einsum(
        patterns[0], cotangent_part, value_part, preferred_element_type=jnp.float32
    )
    spread = jnp.sum(shares * share_grad, axis=-1, keepdims=True)
    score_grad = shares * (share_grad - spread)
    score_half = score_grad.astype(jnp.bfloat16)
    query_grad = (
        jnp.einsum(patterns[1], score_half, key_part, preferred_element_type=jnp.float32) * scaling
    )
    key_grad = (
        jnp.einsum(patterns[2], score_half, query_part, preferred_element_type=jnp.float32)
        * scaling
    )
    return (query_grad, key_grad, value_grad, score_grad)


def quad_step(value, axis, size, step):
    received = [
        lax.ppermute(value, axis, [(index, index ^ (part * step)) for index in range(size)])
        for part in (1, 2, 3)
    ]
    return (value + received[0]) + (received[1] + received[2])


def on_device(queries, keys, values, cotangent, spatial_count, clip_ids, time_bias):
    head_count, frames_all = time_bias.shape
    positions = queries.shape[2]
    width = queries.shape[3]
    seq_size = lax.axis_size("seq")
    dp_size = lax.axis_size("dp")
    row_index = lax.broadcasted_iota(jnp.int32, (frames_all, frames_all), 0)
    col_index = lax.broadcasted_iota(jnp.int32, (frames_all, frames_all), 1)
    distance = jnp.abs(row_index - col_index)
    lag_index = lax.broadcasted_iota(jnp.int32, (frames_all, frames_all, frames_all), 0)
    onehot = (lag_index == distance[None]).astype(jnp.float32)
    bias_table = jnp.tensordot(time_bias, onehot, axes=1, precision=lax.Precision.HIGHEST)[
        None, None
    ]
    same_clip = (clip_ids[:, :, None] == clip_ids[:, None, :])[:, None, None]
    position = lax.broadcasted_iota(jnp.int32, (1, 1, 1, 1, positions), 4)
    live_keys = position < spatial_count[:, :, None, None, None]

    block = positions // seq_size
    stacked = jnp.stack(
        [
            tensor.reshape(seq_size, block, width)
            for tensor in (keys, values, queries, cotangent)
        ],
        axis=2,
    )
    rows = lax.all_to_all(stacked, "seq", split_axis=0, concat_axis=0, tiled=True)
    rows = rows.reshape(seq_size, block, 4, head_count, width // head_count)
    rows = jnp.transpose(rows, (2, 1, 3, 0, 4))
    scaling = 1.0 / math.sqrt(rows.shape[-1])
    pair = jnp.einsum(
        "tphie,tphje->tphij", rows[2:4], rows[0:2], preferred_element_type=jnp.float32
    )
    scores = pair[0] * scaling + bias_table[0]
    scores = jnp.where(same_clip[0], scores, -1e30)
    row_peak = jnp.max(scores, axis=-1, keepdims=True)
    weights = jnp.exp(scores - row_peak)
    shares = weights / jnp.sum(weights, axis=-1, keepdims=True)
    share_grad = pair[1]
    spread = jnp.sum(shares * share_grad, axis=-1, keepdims=True)
    score_grad = shares * (share_grad - spread)
    bias_part = jnp.tensordot(
        jnp.sum(score_grad, axis=0),
        onehot,
        axes=((1, 2), (1, 2)),
        precision=lax.Precision.HIGHEST,
    )
    partial = quad_step(bias_part, "seq", seq_size, 1)
    partial, shares, score_grad, rows = lax.optimization_barrier(
        (partial, shares, score_grad, rows)
    )
    shares_half = shares.astype(jnp.bfloat16)
    score_half = score_grad.astype(jnp.bfloat16)
    mixers = jnp.stack(
        [
            score_half,
            shares_half,
            jnp.swapaxes(score_half, -1, -2),
            jnp.swapaxes(shares_half, -1, -2),
        ]
    )
    outs = jnp.einsum("tphij,tphje->tphie", mixers, rows, preferred_element_type=jnp.float32)
    factor = jnp.array([scaling, 1.0, scaling, 1.0], jnp.float32)[:, None, None, None, None]
    outs = outs * factor
    partial = quad_step(partial, "seq", seq_size, 4)
    back_rows = jnp.transpose(outs.astype(jnp.bfloat16), (3, 1, 0, 2, 4)).reshape(
        seq_size, block, 4, width
    )
    partial, back_rows = lax.optimization_barrier((partial, back_rows))
    summed = quad_step(quad_step(partial, "dp", dp_size, 1), "dp", dp_size, 4)
    bias_grad = summed / math.sqrt(dp_size * queries.shape[0] * frames_all * positions)
    back = lax.all_to_all(back_rows, "seq", split_axis=0, concat_axis=0, tiled=True)
    back = jnp.moveaxis(back, 2, 0).reshape(4, 1, 1, positions, width).astype(jnp.float32)

    space_query = split_heads(queries, head_count)
    space_key = split_heads(keys, head_count)
    space_value = split_heads(values, head_count)
    space_slope = split_heads(cotangent, head_count)
    space_shares, space_half, space_out = attend_forward(
        SPACE_PATTERNS, space_query, space_key, space_value, 0.0, live_keys
    )
    space_grads = attend_backward(
        SPACE_PATTERNS, space_query, space_key, space_value, space_slope, space_shares, space_half
    )
    attended = (join_heads(space_out) + back[1]).astype(jnp.bfloat16)
    query_grad = (join_heads(space_grads[0]) + back[0]).astype(jnp.bfloat16)
    key_grad = (join_heads(space_grads[1]) + back[2]).astype(jnp.bfloat16)
    value_grad = (join_heads(space_grads[2]) + back[3]).astype(jnp.bfloat16)
    return (attended, query_grad, key_grad, value_grad, bias_grad)


def solution(mesh):
    return jax.shard_map(
        on_device,
        mesh=mesh,
        in_specs=(
            P("dp", "seq", None, None),
            P("dp", "seq", None, None),
            P("dp", "seq", None, None),
            P("dp", "seq", None, None),
            P("dp", "seq"),
            P("dp", None),
            P(),
        ),
        out_specs=(
            P("dp", "seq", None, None),
            P("dp", "seq", None, None),
            P("dp", "seq", None, None),
            P("dp", "seq", None, None),
            P(),
        ),
        check_vma=False,
    )
```

```python
import math

import jax
import jax.numpy as jnp
from jax import lax
from jax.sharding import PartitionSpec as P

SPACE_PATTERNS = ("bfihe,bfjhe->bfhij", "bfhij,bfjhe->bfihe", "bfhij,bfihe->bfjhe")
TIME_PATTERNS = ("phie,phje->phij", "phij,phje->phie", "phij,phie->phje")


def split_heads(tensor, head_count):
    return tensor.reshape(tensor.shape[:-1] + (head_count, tensor.shape[-1] // head_count))


def join_heads(tensor):
    return tensor.reshape(tensor.shape[:-2] + (tensor.shape[-2] * tensor.shape[-1],))


def attend_forward(patterns, query_part, key_part, value_part, bias, allowed):
    scaling = 1.0 / math.sqrt(query_part.shape[-1])
    scores = (
        jnp.einsum(patterns[0], query_part, key_part, preferred_element_type=jnp.float32) * scaling
        + bias
    )
    scores = jnp.where(allowed, scores, -1e30)
    row_peak = jnp.max(scores, axis=-1, keepdims=True)
    weights = jnp.exp(scores - row_peak)
    shares = weights / jnp.sum(weights, axis=-1, keepdims=True)
    shares_half = shares.astype(jnp.bfloat16)
    result = jnp.einsum(patterns[1], shares_half, value_part, preferred_element_type=jnp.float32)
    return (shares, shares_half, result)


def attend_backward(
    patterns, query_part, key_part, value_part, cotangent_part, shares, shares_half
):
    scaling = 1.0 / math.sqrt(query_part.shape[-1])
    value_grad = jnp.einsum(
        patterns[2], shares_half, cotangent_part, preferred_element_type=jnp.float32
    )
    share_grad = jnp.einsum(
        patterns[0], cotangent_part, value_part, preferred_element_type=jnp.float32
    )
    spread = jnp.sum(shares * share_grad, axis=-1, keepdims=True)
    score_grad = shares * (share_grad - spread)
    score_half = score_grad.astype(jnp.bfloat16)
    query_grad = (
        jnp.einsum(patterns[1], score_half, key_part, preferred_element_type=jnp.float32) * scaling
    )
    key_grad = (
        jnp.einsum(patterns[2], score_half, query_part, preferred_element_type=jnp.float32)
        * scaling
    )
    return (query_grad, key_grad, value_grad, score_grad)


def quad_step(value, axis, size, step):
    received = [
        lax.ppermute(value, axis, [(index, index ^ (part * step)) for index in range(size)])
        for part in (1, 2, 3)
    ]
    return (value + received[0]) + (received[1] + received[2])


def on_device(queries, keys, values, cotangent, spatial_count, clip_ids, time_bias):
    head_count, frames_all = time_bias.shape
    positions = queries.shape[2]
    width = queries.shape[3]
    seq_size = lax.axis_size("seq")
    dp_size = lax.axis_size("dp")
    row_index = lax.broadcasted_iota(jnp.int32, (frames_all, frames_all), 0)
    col_index = lax.broadcasted_iota(jnp.int32, (frames_all, frames_all), 1)
    distance = jnp.abs(row_index - col_index)
    lag_index = lax.broadcasted_iota(jnp.int32, (frames_all, frames_all, frames_all), 0)
    onehot = (lag_index == distance[None]).astype(jnp.float32)
    bias_table = jnp.tensordot(time_bias, onehot, axes=1, precision=lax.Precision.HIGHEST)[
        None, None
    ]
    same_clip = (clip_ids[:, :, None] == clip_ids[:, None, :])[:, None, None]
    position = lax.broadcasted_iota(jnp.int32, (1, 1, 1, 1, positions), 4)
    live_keys = position < spatial_count[:, :, None, None, None]

    block = positions // seq_size
    stacked = jnp.stack(
        [
            tensor.reshape(seq_size, block, width)
            for tensor in (queries, keys, values, cotangent)
        ],
        axis=2,
    )
    rows = lax.all_to_all(stacked, "seq", split_axis=0, concat_axis=0, tiled=True)
    rows = rows.reshape(seq_size, block, 4, head_count, width // head_count)
    rows = jnp.transpose(rows, (2, 1, 3, 0, 4))
    query_part, key_part, value_part, slope_part = rows[0], rows[1], rows[2], rows[3]
    scaling = 1.0 / math.sqrt(query_part.shape[-1])
    scores = (
        jnp.einsum(TIME_PATTERNS[0], query_part, key_part, preferred_element_type=jnp.float32)
        * scaling
        + bias_table[0]
    )
    scores = jnp.where(same_clip[0], scores, -1e30)
    row_peak = jnp.max(scores, axis=-1, keepdims=True)
    weights = jnp.exp(scores - row_peak)
    shares = weights / jnp.sum(weights, axis=-1, keepdims=True)
    share_grad = jnp.einsum(
        TIME_PATTERNS[0], slope_part, value_part, preferred_element_type=jnp.float32
    )
    spread = jnp.sum(shares * share_grad, axis=-1, keepdims=True)
    score_grad = shares * (share_grad - spread)
    bias_part = jnp.tensordot(
        jnp.sum(score_grad, axis=0),
        onehot,
        axes=((1, 2), (1, 2)),
        precision=lax.Precision.HIGHEST,
    )
    partial = quad_step(bias_part, "seq", seq_size, 1)
    partial, shares, score_grad, query_part, key_part, value_part, slope_part = (
        lax.optimization_barrier(
            (partial, shares, score_grad, query_part, key_part, value_part, slope_part)
        )
    )
    shares_half = shares.astype(jnp.bfloat16)
    score_half = score_grad.astype(jnp.bfloat16)
    result = jnp.einsum(
        TIME_PATTERNS[1], shares_half, value_part, preferred_element_type=jnp.float32
    )
    time_value_grad = jnp.einsum(
        TIME_PATTERNS[2], shares_half, slope_part, preferred_element_type=jnp.float32
    )
    time_query_grad = (
        jnp.einsum(TIME_PATTERNS[1], score_half, key_part, preferred_element_type=jnp.float32)
        * scaling
    )
    time_key_grad = (
        jnp.einsum(TIME_PATTERNS[2], score_half, query_part, preferred_element_type=jnp.float32)
        * scaling
    )
    back_rows = jnp.stack(
        [
            jnp.transpose(tensor.astype(jnp.bfloat16), (2, 0, 1, 3)).reshape(seq_size, block, width)
            for tensor in (result, time_query_grad, time_key_grad, time_value_grad)
        ],
        axis=2,
    )
    partial, back_rows = lax.optimization_barrier((partial, back_rows))
    partial = quad_step(partial, "seq", seq_size, 4)
    summed = quad_step(quad_step(partial, "dp", dp_size, 1), "dp", dp_size, 4)
    bias_grad = summed / math.sqrt(dp_size * queries.shape[0] * frames_all * positions)
    back = lax.all_to_all(back_rows, "seq", split_axis=0, concat_axis=0, tiled=True)
    back = jnp.moveaxis(back, 2, 0).reshape(4, 1, 1, positions, width).astype(jnp.float32)

    space_query = split_heads(queries, head_count)
    space_key = split_heads(keys, head_count)
    space_value = split_heads(values, head_count)
    space_slope = split_heads(cotangent, head_count)
    space_shares, space_half, space_out = attend_forward(
        SPACE_PATTERNS, space_query, space_key, space_value, 0.0, live_keys
    )
    space_grads = attend_backward(
        SPACE_PATTERNS, space_query, space_key, space_value, space_slope, space_shares, space_half
    )
    attended = (join_heads(space_out) + back[0]).astype(jnp.bfloat16)
    query_grad = (join_heads(space_grads[0]) + back[1]).astype(jnp.bfloat16)
    key_grad = (join_heads(space_grads[1]) + back[2]).astype(jnp.bfloat16)
    value_grad = (join_heads(space_grads[2]) + back[3]).astype(jnp.bfloat16)
    return (attended, query_grad, key_grad, value_grad, bias_grad)


def solution(mesh):
    return jax.shard_map(
        on_device,
        mesh=mesh,
        in_specs=(
            P("dp", "seq", None, None),
            P("dp", "seq", None, None),
            P("dp", "seq", None, None),
            P("dp", "seq", None, None),
            P("dp", "seq"),
            P("dp", None),
            P(),
        ),
        out_specs=(
            P("dp", "seq", None, None),
            P("dp", "seq", None, None),
            P("dp", "seq", None, None),
            P("dp", "seq", None, None),
            P(),
        ),
        check_vma=False,
    )
```

```python
import math

import jax
import jax.numpy as jnp
from jax import lax
from jax.sharding import PartitionSpec as P

SPACE_PATTERNS = ("bfihe,bfjhe->bfhij", "bfhij,bfjhe->bfihe", "bfhij,bfihe->bfjhe")
TIME_PATTERNS = ("phie,phje->phij", "phij,phje->phie", "phij,phie->phje")


def split_heads(tensor, head_count):
    return tensor.reshape(tensor.shape[:-1] + (head_count, tensor.shape[-1] // head_count))


def join_heads(tensor):
    return tensor.reshape(tensor.shape[:-2] + (tensor.shape[-2] * tensor.shape[-1],))


def attend_forward(patterns, query_part, key_part, value_part, bias, allowed):
    scaling = 1.0 / math.sqrt(query_part.shape[-1])
    scores = (
        jnp.einsum(patterns[0], query_part, key_part, preferred_element_type=jnp.float32) * scaling
        + bias
    )
    scores = jnp.where(allowed, scores, -1e30)
    row_peak = jnp.max(scores, axis=-1, keepdims=True)
    weights = jnp.exp(scores - row_peak)
    shares = weights / jnp.sum(weights, axis=-1, keepdims=True)
    shares_half = shares.astype(jnp.bfloat16)
    result = jnp.einsum(patterns[1], shares_half, value_part, preferred_element_type=jnp.float32)
    return (shares, shares_half, result)


def attend_backward(
    patterns, query_part, key_part, value_part, cotangent_part, shares, shares_half
):
    scaling = 1.0 / math.sqrt(query_part.shape[-1])
    value_grad = jnp.einsum(
        patterns[2], shares_half, cotangent_part, preferred_element_type=jnp.float32
    )
    share_grad = jnp.einsum(
        patterns[0], cotangent_part, value_part, preferred_element_type=jnp.float32
    )
    spread = jnp.sum(shares * share_grad, axis=-1, keepdims=True)
    score_grad = shares * (share_grad - spread)
    score_half = score_grad.astype(jnp.bfloat16)
    query_grad = (
        jnp.einsum(patterns[1], score_half, key_part, preferred_element_type=jnp.float32) * scaling
    )
    key_grad = (
        jnp.einsum(patterns[2], score_half, query_part, preferred_element_type=jnp.float32)
        * scaling
    )
    return (query_grad, key_grad, value_grad, score_grad)


def quad_step(value, axis, size, step):
    received = [
        lax.ppermute(value, axis, [(index, index ^ (part * step)) for index in range(size)])
        for part in (1, 2, 3)
    ]
    return (value + received[0]) + (received[1] + received[2])


def on_device(queries, keys, values, cotangent, spatial_count, clip_ids, time_bias):
    head_count, frames_all = time_bias.shape
    positions = queries.shape[2]
    width = queries.shape[3]
    seq_size = lax.axis_size("seq")
    dp_size = lax.axis_size("dp")
    row_index = lax.broadcasted_iota(jnp.int32, (frames_all, frames_all), 0)
    col_index = lax.broadcasted_iota(jnp.int32, (frames_all, frames_all), 1)
    distance = jnp.abs(row_index - col_index)
    lag_index = lax.broadcasted_iota(jnp.int32, (frames_all, frames_all, frames_all), 0)
    onehot = (lag_index == distance[None]).astype(jnp.float32)
    bias_table = jnp.tensordot(time_bias, onehot, axes=1, precision=lax.Precision.HIGHEST)[
        None, None
    ]
    same_clip = (clip_ids[:, :, None] == clip_ids[:, None, :])[:, None, None]
    position = lax.broadcasted_iota(jnp.int32, (1, 1, 1, 1, positions), 4)
    live_keys = position < spatial_count[:, :, None, None, None]

    block = positions // seq_size
    stacked = jnp.stack(
        [
            jnp.swapaxes(tensor.reshape(block, seq_size, width), 0, 1)
            for tensor in (queries, keys, values, cotangent)
        ],
        axis=2,
    )
    rows = lax.all_to_all(stacked, "seq", split_axis=0, concat_axis=0, tiled=True)
    rows = rows.reshape(seq_size, block, 4, head_count, width // head_count)
    rows = jnp.transpose(rows, (2, 1, 3, 0, 4))
    query_part, key_part, value_part, slope_part = rows[0], rows[1], rows[2], rows[3]
    scaling = 1.0 / math.sqrt(query_part.shape[-1])
    scores = (
        jnp.einsum(TIME_PATTERNS[0], query_part, key_part, preferred_element_type=jnp.float32)
        * scaling
        + bias_table[0]
    )
    scores = jnp.where(same_clip[0], scores, -1e30)
    row_peak = jnp.max(scores, axis=-1, keepdims=True)
    weights = jnp.exp(scores - row_peak)
    shares = weights / jnp.sum(weights, axis=-1, keepdims=True)
    share_grad = jnp.einsum(
        TIME_PATTERNS[0], slope_part, value_part, preferred_element_type=jnp.float32
    )
    spread = jnp.sum(shares * share_grad, axis=-1, keepdims=True)
    score_grad = shares * (share_grad - spread)
    bias_part = jnp.tensordot(
        jnp.sum(score_grad, axis=0),
        onehot,
        axes=((1, 2), (1, 2)),
        precision=lax.Precision.HIGHEST,
    )
    partial = quad_step(bias_part, "seq", seq_size, 1)
    partial, shares, score_grad, query_part, key_part, value_part, slope_part = (
        lax.optimization_barrier(
            (partial, shares, score_grad, query_part, key_part, value_part, slope_part)
        )
    )
    shares_half = shares.astype(jnp.bfloat16)
    score_half = score_grad.astype(jnp.bfloat16)
    result = jnp.einsum(
        TIME_PATTERNS[1], shares_half, value_part, preferred_element_type=jnp.float32
    )
    time_value_grad = jnp.einsum(
        TIME_PATTERNS[2], shares_half, slope_part, preferred_element_type=jnp.float32
    )
    time_query_grad = (
        jnp.einsum(TIME_PATTERNS[1], score_half, key_part, preferred_element_type=jnp.float32)
        * scaling
    )
    time_key_grad = (
        jnp.einsum(TIME_PATTERNS[2], score_half, query_part, preferred_element_type=jnp.float32)
        * scaling
    )
    partial = quad_step(partial, "seq", seq_size, 4)
    back_rows = jnp.stack(
        [
            jnp.transpose(tensor.astype(jnp.bfloat16), (2, 0, 1, 3)).reshape(seq_size, block, width)
            for tensor in (result, time_query_grad, time_key_grad, time_value_grad)
        ],
        axis=2,
    )
    partial, back_rows = lax.optimization_barrier((partial, back_rows))
    summed = quad_step(quad_step(partial, "dp", dp_size, 1), "dp", dp_size, 4)
    bias_grad = summed / math.sqrt(dp_size * queries.shape[0] * frames_all * positions)
    back = lax.all_to_all(back_rows, "seq", split_axis=0, concat_axis=0, tiled=True)
    back = jnp.transpose(back, (2, 1, 0, 3)).reshape(4, 1, 1, positions, width).astype(jnp.float32)

    space_query = split_heads(queries, head_count)
    space_key = split_heads(keys, head_count)
    space_value = split_heads(values, head_count)
    space_slope = split_heads(cotangent, head_count)
    space_shares, space_half, space_out = attend_forward(
        SPACE_PATTERNS, space_query, space_key, space_value, 0.0, live_keys
    )
    space_grads = attend_backward(
        SPACE_PATTERNS, space_query, space_key, space_value, space_slope, space_shares, space_half
    )
    attended = (join_heads(space_out) + back[0]).astype(jnp.bfloat16)
    query_grad = (join_heads(space_grads[0]) + back[1]).astype(jnp.bfloat16)
    key_grad = (join_heads(space_grads[1]) + back[2]).astype(jnp.bfloat16)
    value_grad = (join_heads(space_grads[2]) + back[3]).astype(jnp.bfloat16)
    return (attended, query_grad, key_grad, value_grad, bias_grad)


def solution(mesh):
    return jax.shard_map(
        on_device,
        mesh=mesh,
        in_specs=(
            P("dp", "seq", None, None),
            P("dp", "seq", None, None),
            P("dp", "seq", None, None),
            P("dp", "seq", None, None),
            P("dp", "seq"),
            P("dp", None),
            P(),
        ),
        out_specs=(
            P("dp", "seq", None, None),
            P("dp", "seq", None, None),
            P("dp", "seq", None, None),
            P("dp", "seq", None, None),
            P(),
        ),
        check_vma=False,
    )
```

```python
import math

import jax
import jax.numpy as jnp
from jax import lax
from jax.sharding import PartitionSpec as P

SPACE_PATTERNS = ("bfihe,bfjhe->bfhij", "bfhij,bfjhe->bfihe", "bfhij,bfihe->bfjhe")
TIME_PATTERNS = ("phie,phje->phij", "phij,phje->phie", "phij,phie->phje")


def split_heads(tensor, head_count):
    return tensor.reshape(tensor.shape[:-1] + (head_count, tensor.shape[-1] // head_count))


def join_heads(tensor):
    return tensor.reshape(tensor.shape[:-2] + (tensor.shape[-2] * tensor.shape[-1],))


def attend_forward(patterns, query_part, key_part, value_part, bias, allowed):
    scaling = 1.0 / math.sqrt(query_part.shape[-1])
    scores = (
        jnp.einsum(patterns[0], query_part, key_part, preferred_element_type=jnp.float32) * scaling
        + bias
    )
    scores = jnp.where(allowed, scores, -1e30)
    row_peak = jnp.max(scores, axis=-1, keepdims=True)
    weights = jnp.exp(scores - row_peak)
    shares = weights / jnp.sum(weights, axis=-1, keepdims=True)
    shares_half = shares.astype(jnp.bfloat16)
    result = jnp.einsum(patterns[1], shares_half, value_part, preferred_element_type=jnp.float32)
    return (shares, shares_half, result)


def attend_backward(
    patterns, query_part, key_part, value_part, cotangent_part, shares, shares_half
):
    scaling = 1.0 / math.sqrt(query_part.shape[-1])
    value_grad = jnp.einsum(
        patterns[2], shares_half, cotangent_part, preferred_element_type=jnp.float32
    )
    share_grad = jnp.einsum(
        patterns[0], cotangent_part, value_part, preferred_element_type=jnp.float32
    )
    spread = jnp.sum(shares * share_grad, axis=-1, keepdims=True)
    score_grad = shares * (share_grad - spread)
    score_half = score_grad.astype(jnp.bfloat16)
    query_grad = (
        jnp.einsum(patterns[1], score_half, key_part, preferred_element_type=jnp.float32) * scaling
    )
    key_grad = (
        jnp.einsum(patterns[2], score_half, query_part, preferred_element_type=jnp.float32)
        * scaling
    )
    return (query_grad, key_grad, value_grad, score_grad)


def quad_step(value, axis, size, step):
    received = [
        lax.ppermute(value, axis, [(index, index ^ (part * step)) for index in range(size)])
        for part in (1, 2, 3)
    ]
    return (value + received[0]) + (received[1] + received[2])


def on_device(queries, keys, values, cotangent, spatial_count, clip_ids, time_bias):
    head_count, frames_all = time_bias.shape
    positions = queries.shape[2]
    width = queries.shape[3]
    seq_size = lax.axis_size("seq")
    dp_size = lax.axis_size("dp")
    row_index = lax.broadcasted_iota(jnp.int32, (frames_all, frames_all), 0)
    col_index = lax.broadcasted_iota(jnp.int32, (frames_all, frames_all), 1)
    distance = jnp.abs(row_index - col_index)
    lag_index = lax.broadcasted_iota(jnp.int32, (frames_all, frames_all, frames_all), 0)
    onehot = (lag_index == distance[None]).astype(jnp.float32)
    bias_table = jnp.tensordot(time_bias, onehot, axes=1, precision=lax.Precision.HIGHEST)[
        None, None
    ]
    same_clip = (clip_ids[:, :, None] == clip_ids[:, None, :])[:, None, None]
    position = lax.broadcasted_iota(jnp.int32, (1, 1, 1, 1, positions), 4)
    live_keys = position < spatial_count[:, :, None, None, None]

    block = positions // seq_size
    stacked = jnp.stack(
        [
            jnp.swapaxes(tensor.reshape(block, seq_size, width), 0, 1)
            for tensor in (queries, keys, values, cotangent)
        ],
        axis=2,
    )
    rows = lax.all_to_all(stacked, "seq", split_axis=0, concat_axis=0, tiled=True)
    rows = rows.reshape(seq_size, block, 4, head_count, width // head_count)
    rows = jnp.transpose(rows, (2, 1, 3, 0, 4))
    query_part, key_part, value_part, slope_part = rows[0], rows[1], rows[2], rows[3]
    scaling = 1.0 / math.sqrt(query_part.shape[-1])
    scores = (
        jnp.einsum(TIME_PATTERNS[0], query_part, key_part, preferred_element_type=jnp.float32)
        * scaling
        + bias_table[0]
    )
    scores = jnp.where(same_clip[0], scores, -1e30)
    row_peak = jnp.max(scores, axis=-1, keepdims=True)
    weights = jnp.exp(scores - row_peak)
    shares = weights / jnp.sum(weights, axis=-1, keepdims=True)
    share_grad = jnp.einsum(
        TIME_PATTERNS[0], slope_part, value_part, preferred_element_type=jnp.float32
    )
    spread = jnp.sum(shares * share_grad, axis=-1, keepdims=True)
    score_grad = shares * (share_grad - spread)
    bias_part = jnp.tensordot(
        jnp.sum(score_grad, axis=0),
        onehot,
        axes=((1, 2), (1, 2)),
        precision=lax.Precision.HIGHEST,
    )
    partial = quad_step(bias_part, "seq", seq_size, 1)
    partial, shares, score_grad, query_part, key_part, value_part, slope_part = (
        lax.optimization_barrier(
            (partial, shares, score_grad, query_part, key_part, value_part, slope_part)
        )
    )
    shares_half = shares.astype(jnp.bfloat16)
    score_half = score_grad.astype(jnp.bfloat16)
    result = jnp.einsum(
        TIME_PATTERNS[1], shares_half, value_part, preferred_element_type=jnp.float32
    )
    time_value_grad = jnp.einsum(
        TIME_PATTERNS[2], shares_half, slope_part, preferred_element_type=jnp.float32
    )
    time_query_grad = (
        jnp.einsum(TIME_PATTERNS[1], score_half, key_part, preferred_element_type=jnp.float32)
        * scaling
    )
    time_key_grad = (
        jnp.einsum(TIME_PATTERNS[2], score_half, query_part, preferred_element_type=jnp.float32)
        * scaling
    )
    partial = quad_step(partial, "seq", seq_size, 4)
    back_rows = jnp.stack(
        [
            jnp.transpose(tensor.astype(jnp.bfloat16), (2, 0, 1, 3)).reshape(seq_size, block, width)
            for tensor in (result, time_query_grad, time_key_grad, time_value_grad)
        ],
        axis=2,
    )
    partial, back_rows = lax.optimization_barrier((partial, back_rows))
    summed = quad_step(quad_step(partial, "dp", dp_size, 1), "dp", dp_size, 4)
    bias_grad = summed / math.sqrt(dp_size * queries.shape[0] * frames_all * positions)
    back = lax.all_to_all(back_rows, "seq", split_axis=0, concat_axis=0, tiled=True)

    space_query = split_heads(queries, head_count)
    space_key = split_heads(keys, head_count)
    space_value = split_heads(values, head_count)
    space_slope = split_heads(cotangent, head_count)
    space_shares, space_half, space_out = attend_forward(
        SPACE_PATTERNS, space_query, space_key, space_value, 0.0, live_keys
    )
    space_grads = attend_backward(
        SPACE_PATTERNS, space_query, space_key, space_value, space_slope, space_shares, space_half
    )
    def combine(space_part, tensor):
        space_rows = join_heads(space_part).reshape(block, seq_size, width)
        total = space_rows + jnp.swapaxes(back[:, :, tensor, :], 0, 1).astype(jnp.float32)
        return total.astype(jnp.bfloat16).reshape(1, 1, positions, width)

    attended = combine(space_out, 0)
    query_grad = combine(space_grads[0], 1)
    key_grad = combine(space_grads[1], 2)
    value_grad = combine(space_grads[2], 3)
    return (attended, query_grad, key_grad, value_grad, bias_grad)


def solution(mesh):
    return jax.shard_map(
        on_device,
        mesh=mesh,
        in_specs=(
            P("dp", "seq", None, None),
            P("dp", "seq", None, None),
            P("dp", "seq", None, None),
            P("dp", "seq", None, None),
            P("dp", "seq"),
            P("dp", None),
            P(),
        ),
        out_specs=(
            P("dp", "seq", None, None),
            P("dp", "seq", None, None),
            P("dp", "seq", None, None),
            P("dp", "seq", None, None),
            P(),
        ),
        check_vma=False,
    )
```

```python
import math

import jax
import jax.numpy as jnp
from jax import lax
from jax.sharding import PartitionSpec as P

SPACE_PATTERNS = ("bfihe,bfjhe->bfhij", "bfhij,bfjhe->bfihe", "bfhij,bfihe->bfjhe")
TIME_PATTERNS = ("phie,phje->phij", "phij,phje->phie", "phij,phie->phje")


def split_heads(tensor, head_count):
    return tensor.reshape(tensor.shape[:-1] + (head_count, tensor.shape[-1] // head_count))


def join_heads(tensor):
    return tensor.reshape(tensor.shape[:-2] + (tensor.shape[-2] * tensor.shape[-1],))


def attend_forward(patterns, query_part, key_part, value_part, bias, allowed):
    scaling = 1.0 / math.sqrt(query_part.shape[-1])
    scores = (
        jnp.einsum(patterns[0], query_part, key_part, preferred_element_type=jnp.float32) * scaling
        + bias
    )
    scores = jnp.where(allowed, scores, -1e30)
    row_peak = jnp.max(scores, axis=-1, keepdims=True)
    weights = jnp.exp(scores - row_peak)
    shares = weights / jnp.sum(weights, axis=-1, keepdims=True)
    shares_half = shares.astype(jnp.bfloat16)
    result = jnp.einsum(patterns[1], shares_half, value_part, preferred_element_type=jnp.float32)
    return (shares, shares_half, result)


def attend_backward(
    patterns, query_part, key_part, value_part, cotangent_part, shares, shares_half
):
    scaling = 1.0 / math.sqrt(query_part.shape[-1])
    value_grad = jnp.einsum(
        patterns[2], shares_half, cotangent_part, preferred_element_type=jnp.float32
    )
    share_grad = jnp.einsum(
        patterns[0], cotangent_part, value_part, preferred_element_type=jnp.float32
    )
    spread = jnp.sum(shares * share_grad, axis=-1, keepdims=True)
    score_grad = shares * (share_grad - spread)
    score_half = score_grad.astype(jnp.bfloat16)
    query_grad = (
        jnp.einsum(patterns[1], score_half, key_part, preferred_element_type=jnp.float32) * scaling
    )
    key_grad = (
        jnp.einsum(patterns[2], score_half, query_part, preferred_element_type=jnp.float32)
        * scaling
    )
    return (query_grad, key_grad, value_grad, score_grad)


def quad_step(value, axis, size, step):
    received = [
        lax.ppermute(value, axis, [(index, index ^ (part * step)) for index in range(size)])
        for part in (1, 2, 3)
    ]
    return (value + received[0]) + (received[1] + received[2])


def on_device(queries, keys, values, cotangent, spatial_count, clip_ids, time_bias):
    head_count, frames_all = time_bias.shape
    positions = queries.shape[2]
    width = queries.shape[3]
    seq_size = lax.axis_size("seq")
    dp_size = lax.axis_size("dp")
    row_index = lax.broadcasted_iota(jnp.int32, (frames_all, frames_all), 0)
    col_index = lax.broadcasted_iota(jnp.int32, (frames_all, frames_all), 1)
    distance = jnp.abs(row_index - col_index)
    lag_index = lax.broadcasted_iota(jnp.int32, (frames_all, frames_all, frames_all), 0)
    onehot = (lag_index == distance[None]).astype(jnp.float32)
    bias_table = jnp.tensordot(time_bias, onehot, axes=1, precision=lax.Precision.HIGHEST)[
        None, None
    ]
    same_clip = (clip_ids[:, :, None] == clip_ids[:, None, :])[:, None, None]
    position = lax.broadcasted_iota(jnp.int32, (1, 1, 1, 1, positions), 4)
    live_keys = position < spatial_count[:, :, None, None, None]

    block = positions // seq_size
    stacked = jnp.stack(
        [
            jnp.swapaxes(tensor.reshape(block, seq_size, width), 0, 1)
            for tensor in (queries, keys, values, cotangent)
        ],
        axis=2,
    )
    rows = lax.all_to_all(stacked, "seq", split_axis=0, concat_axis=0, tiled=True)
    rows = rows.reshape(seq_size, block, 4, head_count, width // head_count)
    rows = jnp.transpose(rows, (2, 1, 3, 0, 4))
    query_part, key_part, value_part, slope_part = rows[0], rows[1], rows[2], rows[3]
    scaling = 1.0 / math.sqrt(query_part.shape[-1])
    scores = (
        jnp.einsum(TIME_PATTERNS[0], query_part, key_part, preferred_element_type=jnp.float32)
        * scaling
        + bias_table[0]
    )
    scores = jnp.where(same_clip[0], scores, -1e30)
    row_peak = jnp.max(scores, axis=-1, keepdims=True)
    weights = jnp.exp(scores - row_peak)
    shares = weights / jnp.sum(weights, axis=-1, keepdims=True)
    share_grad = jnp.einsum(
        TIME_PATTERNS[0], slope_part, value_part, preferred_element_type=jnp.float32
    )
    spread = jnp.sum(shares * share_grad, axis=-1, keepdims=True)
    score_grad = shares * (share_grad - spread)
    bias_part = jnp.tensordot(
        jnp.sum(score_grad, axis=0),
        onehot,
        axes=((1, 2), (1, 2)),
        precision=lax.Precision.HIGHEST,
    )
    partial = quad_step(bias_part, "seq", seq_size, 1)
    partial, shares, score_grad, query_part, key_part, value_part, slope_part = (
        lax.optimization_barrier(
            (partial, shares, score_grad, query_part, key_part, value_part, slope_part)
        )
    )
    shares_half = shares.astype(jnp.bfloat16)
    score_half = score_grad.astype(jnp.bfloat16)
    result = jnp.einsum(
        TIME_PATTERNS[1], shares_half, value_part, preferred_element_type=jnp.float32
    )
    time_value_grad = jnp.einsum(
        TIME_PATTERNS[2], shares_half, slope_part, preferred_element_type=jnp.float32
    )
    time_query_grad = (
        jnp.einsum(TIME_PATTERNS[1], score_half, key_part, preferred_element_type=jnp.float32)
        * scaling
    )
    time_key_grad = (
        jnp.einsum(TIME_PATTERNS[2], score_half, query_part, preferred_element_type=jnp.float32)
        * scaling
    )
    partial = quad_step(partial, "seq", seq_size, 4)
    back_rows = jnp.stack(
        [
            jnp.transpose(tensor.astype(jnp.bfloat16), (2, 0, 1, 3)).reshape(seq_size, block, width)
            for tensor in (result, time_query_grad, time_key_grad, time_value_grad)
        ],
        axis=2,
    )
    partial, back_rows = lax.optimization_barrier((partial, back_rows))
    summed = quad_step(quad_step(partial, "dp", dp_size, 1), "dp", dp_size, 4)
    bias_grad = summed / math.sqrt(dp_size * queries.shape[0] * frames_all * positions)
    back = lax.all_to_all(back_rows, "seq", split_axis=0, concat_axis=0, tiled=True)
    back = lax.optimization_barrier(jnp.transpose(back, (2, 1, 0, 3)))
    back = back.reshape(4, 1, 1, positions, width).astype(jnp.float32)

    space_query = split_heads(queries, head_count)
    space_key = split_heads(keys, head_count)
    space_value = split_heads(values, head_count)
    space_slope = split_heads(cotangent, head_count)
    space_shares, space_half, space_out = attend_forward(
        SPACE_PATTERNS, space_query, space_key, space_value, 0.0, live_keys
    )
    space_grads = attend_backward(
        SPACE_PATTERNS, space_query, space_key, space_value, space_slope, space_shares, space_half
    )
    attended = (join_heads(space_out) + back[0]).astype(jnp.bfloat16)
    query_grad = (join_heads(space_grads[0]) + back[1]).astype(jnp.bfloat16)
    key_grad = (join_heads(space_grads[1]) + back[2]).astype(jnp.bfloat16)
    value_grad = (join_heads(space_grads[2]) + back[3]).astype(jnp.bfloat16)
    return (attended, query_grad, key_grad, value_grad, bias_grad)


def solution(mesh):
    return jax.shard_map(
        on_device,
        mesh=mesh,
        in_specs=(
            P("dp", "seq", None, None),
            P("dp", "seq", None, None),
            P("dp", "seq", None, None),
            P("dp", "seq", None, None),
            P("dp", "seq"),
            P("dp", None),
            P(),
        ),
        out_specs=(
            P("dp", "seq", None, None),
            P("dp", "seq", None, None),
            P("dp", "seq", None, None),
            P("dp", "seq", None, None),
            P(),
        ),
        check_vma=False,
    )
```
